256 devices in a mesh: bxy: 32 (over x, z), bz: 8 (over y, core).
Axes of the slice: x: 4, y: 4, z: 8, core: 2. Of those that a mesh axis runs over, the one named last changes fastest.
Arguments:
- basis: float32 [48, 983040], P(None, ('bxy', 'bz')), may hold values from -12 to 12
- velocity: float32 [3, 32, 48, 128], P(None, 'bxy'), may hold values from -0.2 to 0.2
- temper: float32 [32, 48, 128], P('bxy'), may hold values from 0.5 to 1.5
- flags: int32 [32, 48, 128], P('bxy'), may hold values 0 or 1
- order: int32 [32, 30720], P('bxy'), may hold values from 0 to 30719, each once within a row
Outputs:
- ortho: float32 [16, 983040], P(None, ('bxy', 'bz'))
- proj: float32 [48, 16], replicated
- upper: float32 [16, 16], replicated
The draws below stay inside these ranges and needn't reach their ends.
Inputs may be any that keep to these rules, and one draw needn't show every extreme that they name: `order`: for each slab, a permutation of its 30720 local rows.
All inputs are finite; a program needn't handle non-finite values. No bound on the sum of `flags` on one device may be relied on, other than what follows from the above.
Results may differ from the reference program's by a relative error of at most 0.0003.
Values sent between devices are 32-bit elements; how exact they have to be, the bound alone decides.
No kernel may reach another device: no remote copies, remote signals or barrier semaphores. Data moves between devices by JAX's collectives and lax.ppermute only.
A program may use at most 128 MiB of HBM per device.

```python
import math
import jax
import jax.numpy as jnp
from jax import lax

CX = 1
NZ = 48
CY = 128
BLK = 16
KB = 48
STEPS = 2
NX = 32
SLAB_ROWS = 30720
MROWS = 983040
N_BXY = 32
N_BZ = 8


def draw_basis(key, part):
    first, second = jax.random.split(key, 2)
    levels = jax.random.uniform(second, (1, MROWS), minval=0.0, maxval=math.log(10.0))
    scales = jnp.exp(levels) / 4.6
    raw = jax.random.normal(first, (KB, MROWS))
    return jnp.clip(raw * scales, -12.0, 12.0).astype(jnp.float32)


def set_ends(drawn, own_key, least, largest):
    shape = drawn.shape
    index_at = [jax.random.randint(jax.random.fold_in(own_key, axis), (), 0, shape[axis]) for axis in range(len(shape))]
    drawn = drawn.at[tuple(index_at)].set(least)
    longest = shape.index(max(shape))
    index_at[longest] = (index_at[longest] + 1) % shape[longest]
    return drawn.at[tuple(index_at)].set(largest)


def shard_levels(stream_key, dims, shards, smallest, largest):
    level, own = 1.0, jax.random.fold_in(stream_key, 6)
    for position, shards_of in shards:
        heights = jnp.exp(jax.random.uniform(jax.random.fold_in(own, position), (shards_of,), jnp.float32, smallest / len(shards), largest / len(shards)))
        level = level * jnp.repeat(heights, dims[position] // shards_of).reshape([-1 if axis == position else 1 for axis in range(len(dims))])
    return level


def scatter_about(stream_key, extent, deviation, reach, shards=(), kind=jnp.bfloat16):
    values = deviation * jax.random.normal(stream_key, extent, jnp.float32)
    if shards:
        values = values * shard_levels(stream_key, extent, shards, -0.22, 0.18)
    return jnp.clip(values, -reach, reach).astype(kind)


def setup_inputs(seed: int = 0) -> dict:
    arg_keys = jax.random.split(jax.random.key(seed), 6)
    return {
        "basis": draw_basis(jax.random.fold_in(arg_keys[5], 71), 0),
        "velocity": scatter_about(arg_keys[1], (3, NX, NZ, CY), 0.06, 0.2, ((1, 32),), jnp.float32),
        "temper": jnp.clip(0.5 + 1.0 * jax.random.uniform(arg_keys[2], (NX, NZ, CY), jnp.float32) ** shard_levels(arg_keys[2], (NX, NZ, CY), ((0, 32),), -0.2, 0.2), 0.5, 1.5),
        "flags": set_ends((jax.random.randint(arg_keys[3], (NX, NZ, CY), 0, 12) < 1).astype(jnp.int32), jax.random.fold_in(arg_keys[3], 1), 0, 1),
        "order": jax.vmap(lambda own: jax.random.permutation(own, SLAB_ROWS))(jax.random.split(arg_keys[4], N_BXY)).reshape((N_BXY, SLAB_ROWS)).astype(jnp.int32),
    }


FLOW_DIRS = ((0, 0, 0), (1, 0, 0), (-1, 0, 0), (0, 1, 0), (0, -1, 0), (0, 0, 1), (0, 0, -1), (1, 1, 0), (-1, -1, 0), (1, -1, 0), (-1, 1, 0), (1, 0, 1), (-1, 0, -1), (1, 0, -1), (-1, 0, 1), (0, 1, 1), (0, -1, -1), (0, 1, -1), (0, -1, 1))
FLOW_WEIGHTS = (1.0 / 3.0,) + (1.0 / 18.0,) * 6 + (1.0 / 36.0,) * 12
HEAT_WEIGHTS = (0.25,) + (0.125,) * 6
OPPOSITE = (0,) + tuple((number + 1 if number % 2 == 1 else number - 1 for number in range(1, 19)))
OMEGA_FLOW = 1.6
OMEGA_HEAT = 1.4
BUOYANCY = 0.2

def along(direction, comps):
    total = 0.0
    for weight, array in zip(direction, comps):
        if weight == 1:
            total = total + array
        elif weight == -1:
            total = total - array
    return total

def moments(flow, heat):
    density = flow[0]
    for number in range(1, 19):
        density = density + flow[number]
    momentum = []
    for comp in range(3):
        momentum.append(along([FLOW_DIRS[number][comp] for number in range(19)], flow))
    warmth = heat[0]
    for number in range(1, 7):
        warmth = warmth + heat[number]
    return (density, momentum, warmth)

def equilibria(density, momentum, warmth, velocity, temper):
    carried = [momentum[comp] - velocity[comp] * density for comp in range(3)]
    speed_sq = velocity[0] * velocity[0] + velocity[1] * velocity[1] + velocity[2] * velocity[2]
    carried_u = velocity[0] * carried[0] + velocity[1] * carried[1] + velocity[2] * carried[2]
    flow_eq = []
    heat_eq = []
    for number in range(19):
        drift = along(FLOW_DIRS[number], velocity)
        push = along(FLOW_DIRS[number], carried)
        value = density * (1.0 + 3.0 * drift + 4.5 * drift * drift - 1.5 * speed_sq) + 3.0 * push + 9.0 * drift * push - 3.0 * carried_u
        flow_eq.append(FLOW_WEIGHTS[number] * value)
        if number < 7:
            heat_eq.append(HEAT_WEIGHTS[number] * (warmth * (1.0 + 4.0 * drift) + 4.0 * temper * push))
    return (flow_eq, heat_eq)

def collide(flow, heat, velocity, temper, solid):
    density, momentum, warmth = moments(flow, heat)
    flow_eq, heat_eq = equilibria(density, momentum, warmth, velocity, temper)
    flow_new = []
    heat_new = []
    for number in range(19):
        fresh = flow[number] - OMEGA_FLOW * (flow[number] - flow_eq[number]) + 3.0 * FLOW_WEIGHTS[number] * FLOW_DIRS[number][1] * BUOYANCY * warmth
        flow_new.append(jnp.where(solid, flow[OPPOSITE[number]], fresh))
    for number in range(7):
        fresh = heat[number] - OMEGA_HEAT * (heat[number] - heat_eq[number])
        heat_new.append(jnp.where(solid, heat[OPPOSITE[number]], fresh))
    return (flow_new, heat_new)

def reference(basis, velocity, temper, flags, order):
    devices = N_BXY * N_BZ
    piece_rows = SLAB_ROWS // devices
    slab_order = order.astype(jnp.int32)
    counter = jnp.arange(SLAB_ROWS, dtype=jnp.int32)
    inverse = jax.vmap(lambda row: jnp.zeros((SLAB_ROWS,), jnp.int32).at[row].set(counter))(slab_order)
    block = basis[KB - BLK:]
    permuted = block.reshape(BLK, devices, N_BXY, piece_rows).transpose(0, 2, 1, 3).reshape(BLK, N_BXY, SLAB_ROWS)
    slabs = jnp.take_along_axis(permuted, jnp.broadcast_to(inverse[None], permuted.shape), axis=2)
    fields = slabs.reshape(BLK, N_BXY, 5, CX, NZ, CY).transpose(0, 2, 1, 3, 4, 5).reshape(BLK, 5, NX, NZ, CY)
    height = lax.broadcasted_iota(jnp.int32, (NX, NZ, CY), 1)
    solid = (flags == 1) | (height == 0) | (height == NZ - 1)
    speeds = [velocity[0], velocity[1], velocity[2]]

    def evolve(field):
        flow, heat = equilibria(field[0], [field[1], field[2], field[3]], field[4], speeds, temper)
        for turn in range(STEPS):
            flow, heat = collide(flow, heat, speeds, temper, solid)
            flow = [jnp.roll(flow[number], FLOW_DIRS[number], axis=(0, 1, 2)) for number in range(19)]
            heat = [jnp.roll(heat[number], FLOW_DIRS[number], axis=(0, 1, 2)) for number in range(7)]
        density, momentum, warmth = moments(flow, heat)
        return jnp.stack([density] + momentum + [warmth], 0)
    evolved = lax.map(evolve, fields)
    back = evolved.reshape(BLK, 5, N_BXY, CX, NZ, CY).transpose(0, 2, 1, 3, 4, 5).reshape(BLK, N_BXY, SLAB_ROWS)
    reordered = jnp.take_along_axis(back, jnp.broadcast_to(slab_order[None], back.shape), axis=2)
    work = reordered.reshape(BLK, N_BXY, devices, piece_rows).transpose(0, 2, 1, 3).reshape(BLK, MROWS)
    highest = lax.Precision.HIGHEST
    proj = jnp.dot(basis, work.T, precision=highest) / MROWS
    resid = work - jnp.dot(proj.T, basis, precision=highest)
    gram = jnp.dot(resid, resid.T, precision=highest) / MROWS
    lower = jnp.linalg.cholesky(gram)
    ortho = lax.linalg.triangular_solve(lower, resid, left_side=True, lower=True)
    return (ortho, proj, lower.T)
```

```python
import jax
import jax.numpy as jnp
from jax import lax
from jax.sharding import PartitionSpec as P

BLK = 16
KB = 48
STEPS = 2


FLOW_DIRS = (
    (0, 0, 0),
    (1, 0, 0),
    (-1, 0, 0),
    (0, 1, 0),
    (0, -1, 0),
    (0, 0, 1),
    (0, 0, -1),
    (1, 1, 0),
    (-1, -1, 0),
    (1, -1, 0),
    (-1, 1, 0),
    (1, 0, 1),
    (-1, 0, -1),
    (1, 0, -1),
    (-1, 0, 1),
    (0, 1, 1),
    (0, -1, -1),
    (0, 1, -1),
    (0, -1, 1),
)
ALL_DIRS = FLOW_DIRS + FLOW_DIRS[:7]
FLOW_WEIGHTS = (1.0 / 3.0,) + (1.0 / 18.0,) * 6 + (1.0 / 36.0,) * 12
HEAT_WEIGHTS = (0.25,) + (0.125,) * 6
OPPOSITE = (0,) + tuple((number + 1 if number % 2 == 1 else number - 1 for number in range(1, 19)))
OMEGA_FLOW = 1.6
OMEGA_HEAT = 1.4
BUOYANCY = 0.2


def with_halo(block, sides, width):
    for axis, dim in sides:
        count = lax.axis_size(axis)
        forward = [(i, i + 1) for i in range(count - 1)]
        forward.append((count - 1, 0))
        backward = [(target, source) for source, target in forward]
        low = lax.ppermute(
            lax.slice_in_dim(block, block.shape[dim] - width, None, axis=dim), axis, forward
        )
        high = lax.ppermute(lax.slice_in_dim(block, 0, width, axis=dim), axis, backward)
        block = jnp.concatenate([low, block, high], axis=dim)
    return block


def tree_sum(value, axes):
    for axis in axes:
        count = lax.axis_size(axis)
        if count & (count - 1):
            value = lax.psum(value, axis)
            continue
        stride = 1
        while stride < count:
            value = value + lax.ppermute(value, axis, [(i, i ^ stride) for i in range(count)])
            stride *= 2
    return value


def along(direction, comps):
    total = 0.0
    for weight, array in zip(direction, comps):
        if weight == 1:
            total = total + array
        elif weight == -1:
            total = total - array
    return total


def moments(flow, heat):
    density = flow[0]
    for number in range(1, 19):
        density = density + flow[number]
    momentum = []
    for comp in range(3):
        momentum.append(along([FLOW_DIRS[number][comp] for number in range(19)], flow))
    warmth = heat[0]
    for number in range(1, 7):
        warmth = warmth + heat[number]
    return (density, momentum, warmth)


def equilibria(density, momentum, warmth, velocity, temper):
    carried = [momentum[comp] - velocity[comp] * density for comp in range(3)]
    speed_sq = velocity[0] * velocity[0] + velocity[1] * velocity[1] + velocity[2] * velocity[2]
    carried_u = velocity[0] * carried[0] + velocity[1] * carried[1] + velocity[2] * carried[2]
    flow_eq = []
    heat_eq = []
    for number in range(19):
        drift = along(FLOW_DIRS[number], velocity)
        push = along(FLOW_DIRS[number], carried)
        value = (
            density * (1.0 + 3.0 * drift + 4.5 * drift * drift - 1.5 * speed_sq)
            + 3.0 * push
            + 9.0 * drift * push
            - 3.0 * carried_u
        )
        flow_eq.append(FLOW_WEIGHTS[number] * value)
        if number < 7:
            heat_eq.append(
                HEAT_WEIGHTS[number] * (warmth * (1.0 + 4.0 * drift) + 4.0 * temper * push)
            )
    return (flow_eq, heat_eq)


def collide(flow, heat, velocity, temper, solid):
    density, momentum, warmth = moments(flow, heat)
    flow_eq, heat_eq = equilibria(density, momentum, warmth, velocity, temper)
    flow_new = []
    heat_new = []
    for number in range(19):
        fresh = (
            flow[number]
            - OMEGA_FLOW * (flow[number] - flow_eq[number])
            + 3.0 * FLOW_WEIGHTS[number] * FLOW_DIRS[number][1] * BUOYANCY * warmth
        )
        flow_new.append(jnp.where(solid, flow[OPPOSITE[number]], fresh))
    for number in range(7):
        fresh = heat[number] - OMEGA_HEAT * (heat[number] - heat_eq[number])
        heat_new.append(jnp.where(solid, heat[OPPOSITE[number]], fresh))
    return (flow_new, heat_new)


def stream(flow, heat):
    stacked = jnp.stack(flow + heat, 1)
    cells_first = stacked.shape[2]
    padded = with_halo(stacked, (("bxy", 2),), 1)
    moved = []
    for number in range(26):
        first, second, third = ALL_DIRS[number]
        piece = padded[:, number, 1 - first : 1 - first + cells_first]
        moved.append(jnp.roll(piece, (second, third), axis=(2, 3)))
    return (moved[:19], moved[19:])


def body(basis, velocity, temper, flags, order):
    count_first = lax.axis_size("bxy")
    count_second = lax.axis_size("bz")
    devices = count_first * count_second
    panel_rows = basis.shape[1]
    piece_rows = panel_rows // count_first
    slab_rows = piece_rows * devices
    total_rows = panel_rows * devices
    vectors = BLK // count_second
    cells_first, cells_vertical, cells_third = temper.shape
    permute = order.reshape(slab_rows)
    block = basis[KB - BLK :]
    outgoing = (
        block.reshape(count_second, vectors, count_first, piece_rows)
        .transpose(2, 0, 1, 3)
        .reshape(count_first, count_second, vectors * piece_rows)
    )
    arrived = lax.all_to_all(
        lax.all_to_all(outgoing, "bxy", split_axis=0, concat_axis=0, tiled=True),
        "bz",
        split_axis=1,
        concat_axis=1,
        tiled=True,
    )
    permuted = (
        arrived.reshape(devices, vectors, piece_rows).transpose(1, 0, 2).reshape(vectors, slab_rows)
    )
    ranked = lax.sort(
        (permute, lax.iota(jnp.int32, slab_rows)) + tuple(permuted[v] for v in range(vectors)),
        num_keys=1,
    )
    inverse = ranked[1]
    fields = jnp.stack(ranked[2:], 0).reshape(vectors, 5, cells_first, cells_vertical, cells_third)
    height = lax.broadcasted_iota(jnp.int32, temper.shape, 1)
    solid = (flags == 1) | (height == 0) | (height == cells_vertical - 1)
    speeds = [velocity[0], velocity[1], velocity[2]]
    flow, heat = equilibria(
        fields[:, 0], [fields[:, 1], fields[:, 2], fields[:, 3]], fields[:, 4], speeds, temper
    )
    for turn in range(STEPS):
        flow, heat = collide(flow, heat, speeds, temper, solid)
        flow, heat = stream(flow, heat)
    density, momentum, warmth = moments(flow, heat)
    evolved = jnp.stack([density] + momentum + [warmth], 1).reshape(vectors, slab_rows)
    reordered = jnp.stack(
        lax.sort((inverse,) + tuple(evolved[v] for v in range(vectors)), num_keys=1)[1:], 0
    )
    leaving = (
        reordered.reshape(vectors, devices, piece_rows)
        .transpose(1, 0, 2)
        .reshape(count_first, count_second, vectors * piece_rows)
    )
    landed = lax.all_to_all(
        lax.all_to_all(leaving, "bxy", split_axis=0, concat_axis=0, tiled=True),
        "bz",
        split_axis=1,
        concat_axis=1,
        tiled=True,
    )
    work = (
        landed.reshape(count_first, count_second, vectors, piece_rows)
        .transpose(1, 2, 0, 3)
        .reshape(BLK, panel_rows)
    )
    highest = lax.Precision.HIGHEST
    proj = tree_sum(jnp.dot(basis, work.T, precision=highest), ("bz", "bxy")) / total_rows
    resid = work - jnp.dot(proj.T, basis, precision=highest)
    gram = tree_sum(jnp.dot(resid, resid.T, precision=highest), ("bz", "bxy")) / total_rows
    lower = jnp.linalg.cholesky(gram)
    ortho = lax.linalg.triangular_solve(lower, resid, left_side=True, lower=True)
    return (ortho, proj, lower.T)


def solution(mesh):
    in_specs = (
        P(None, ("bxy", "bz")),
        P(None, "bxy", None, None),
        P("bxy", None, None),
        P("bxy", None, None),
        P("bxy", None),
    )
    out_specs = (P(None, ("bxy", "bz")), P(), P())
    return jax.shard_map(body, mesh=mesh, in_specs=in_specs, out_specs=out_specs, check_vma=False)
```

```python
import jax
import jax.numpy as jnp
from jax import lax
from jax.sharding import PartitionSpec as P

BLK = 16
KB = 48
STEPS = 2


FLOW_DIRS = (
    (0, 0, 0),
    (1, 0, 0),
    (-1, 0, 0),
    (0, 1, 0),
    (0, -1, 0),
    (0, 0, 1),
    (0, 0, -1),
    (1, 1, 0),
    (-1, -1, 0),
    (1, -1, 0),
    (-1, 1, 0),
    (1, 0, 1),
    (-1, 0, -1),
    (1, 0, -1),
    (-1, 0, 1),
    (0, 1, 1),
    (0, -1, -1),
    (0, 1, -1),
    (0, -1, 1),
)
ALL_DIRS = FLOW_DIRS + FLOW_DIRS[:7]
FLOW_WEIGHTS = (1.0 / 3.0,) + (1.0 / 18.0,) * 6 + (1.0 / 36.0,) * 12
HEAT_WEIGHTS = (0.25,) + (0.125,) * 6
OPPOSITE = (0,) + tuple((number + 1 if number % 2 == 1 else number - 1 for number in range(1, 19)))
OMEGA_FLOW = 1.6
OMEGA_HEAT = 1.4
BUOYANCY = 0.2


def with_halo(block, sides, width):
    for axis, dim in sides:
        count = lax.axis_size(axis)
        forward = [(i, i + 1) for i in range(count - 1)]
        forward.append((count - 1, 0))
        backward = [(target, source) for source, target in forward]
        low = lax.ppermute(
            lax.slice_in_dim(block, block.shape[dim] - width, None, axis=dim), axis, forward
        )
        high = lax.ppermute(lax.slice_in_dim(block, 0, width, axis=dim), axis, backward)
        block = jnp.concatenate([low, block, high], axis=dim)
    return block


def tree_sum(value, axes):
    for axis in axes:
        count = lax.axis_size(axis)
        if count & (count - 1):
            value = lax.psum(value, axis)
            continue
        stride = 1
        while stride < count:
            value = value + lax.ppermute(value, axis, [(i, i ^ stride) for i in range(count)])
            stride *= 2
    return value


def along(direction, comps):
    total = 0.0
    for weight, array in zip(direction, comps):
        if weight == 1:
            total = total + array
        elif weight == -1:
            total = total - array
    return total


def moments(flow, heat):
    density = flow[0]
    for number in range(1, 19):
        density = density + flow[number]
    momentum = []
    for comp in range(3):
        momentum.append(along([FLOW_DIRS[number][comp] for number in range(19)], flow))
    warmth = heat[0]
    for number in range(1, 7):
        warmth = warmth + heat[number]
    return (density, momentum, warmth)


def equilibria(density, momentum, warmth, velocity, temper):
    carried = [momentum[comp] - velocity[comp] * density for comp in range(3)]
    speed_sq = velocity[0] * velocity[0] + velocity[1] * velocity[1] + velocity[2] * velocity[2]
    carried_u = velocity[0] * carried[0] + velocity[1] * carried[1] + velocity[2] * carried[2]
    flow_eq = []
    heat_eq = []
    for number in range(19):
        drift = along(FLOW_DIRS[number], velocity)
        push = along(FLOW_DIRS[number], carried)
        value = (
            density * (1.0 + 3.0 * drift + 4.5 * drift * drift - 1.5 * speed_sq)
            + 3.0 * push
            + 9.0 * drift * push
            - 3.0 * carried_u
        )
        flow_eq.append(FLOW_WEIGHTS[number] * value)
        if number < 7:
            heat_eq.append(
                HEAT_WEIGHTS[number] * (warmth * (1.0 + 4.0 * drift) + 4.0 * temper * push)
            )
    return (flow_eq, heat_eq)


def collide(flow, heat, velocity, temper, solid):
    density, momentum, warmth = moments(flow, heat)
    flow_eq, heat_eq = equilibria(density, momentum, warmth, velocity, temper)
    flow_new = []
    heat_new = []
    for number in range(19):
        fresh = (
            flow[number]
            - OMEGA_FLOW * (flow[number] - flow_eq[number])
            + 3.0 * FLOW_WEIGHTS[number] * FLOW_DIRS[number][1] * BUOYANCY * warmth
        )
        flow_new.append(jnp.where(solid, flow[OPPOSITE[number]], fresh))
    for number in range(7):
        fresh = heat[number] - OMEGA_HEAT * (heat[number] - heat_eq[number])
        heat_new.append(jnp.where(solid, heat[OPPOSITE[number]], fresh))
    return (flow_new, heat_new)


def stream(flow, heat):
    pops = flow + heat
    cells_first = pops[0].shape[1]
    count = lax.axis_size("bxy")
    forward = [(i, (i + 1) % count) for i in range(count)]
    backward = [((i + 1) % count, i) for i in range(count)]
    plus = [n for n in range(26) if ALL_DIRS[n][0] == 1]
    minus = [n for n in range(26) if ALL_DIRS[n][0] == -1]
    low = lax.ppermute(
        jnp.stack([pops[n][:, cells_first - 1 :] for n in plus], 1), "bxy", forward
    )
    high = lax.ppermute(jnp.stack([pops[n][:, :1] for n in minus], 1), "bxy", backward)
    moved = []
    for number in range(26):
        first, second, third = ALL_DIRS[number]
        piece = pops[number]
        if first == 1:
            piece = jnp.concatenate([low[:, plus.index(number)], piece[:, : cells_first - 1]], 1)
        elif first == -1:
            piece = jnp.concatenate([piece[:, 1:], high[:, minus.index(number)]], 1)
        moved.append(jnp.roll(piece, (second, third), axis=(2, 3)))
    return (moved[:19], moved[19:])


def body(basis, velocity, temper, flags, order):
    count_first = lax.axis_size("bxy")
    count_second = lax.axis_size("bz")
    devices = count_first * count_second
    panel_rows = basis.shape[1]
    piece_rows = panel_rows // count_first
    slab_rows = piece_rows * devices
    total_rows = panel_rows * devices
    vectors = BLK // count_second
    cells_first, cells_vertical, cells_third = temper.shape
    permute = order.reshape(slab_rows)
    block = basis[KB - BLK :]
    outgoing = (
        block.reshape(count_second, vectors, count_first, piece_rows)
        .transpose(2, 0, 1, 3)
        .reshape(count_first, count_second, vectors * piece_rows)
    )
    arrived = lax.all_to_all(
        lax.all_to_all(outgoing, "bxy", split_axis=0, concat_axis=0, tiled=True),
        "bz",
        split_axis=1,
        concat_axis=1,
        tiled=True,
    )
    permuted = (
        arrived.reshape(devices, vectors, piece_rows).transpose(1, 0, 2).reshape(vectors, slab_rows)
    )
    ranked = lax.sort(
        (permute, lax.iota(jnp.int32, slab_rows)) + tuple(permuted[v] for v in range(vectors)),
        num_keys=1,
    )
    inverse = ranked[1]
    fields = jnp.stack(ranked[2:], 0).reshape(vectors, 5, cells_first, cells_vertical, cells_third)
    height = lax.broadcasted_iota(jnp.int32, temper.shape, 1)
    solid = (flags == 1) | (height == 0) | (height == cells_vertical - 1)
    speeds = [velocity[0], velocity[1], velocity[2]]
    flow, heat = equilibria(
        fields[:, 0], [fields[:, 1], fields[:, 2], fields[:, 3]], fields[:, 4], speeds, temper
    )
    for turn in range(STEPS):
        flow, heat = collide(flow, heat, speeds, temper, solid)
        flow, heat = stream(flow, heat)
    density, momentum, warmth = moments(flow, heat)
    evolved = jnp.stack([density] + momentum + [warmth], 1).reshape(vectors, slab_rows)
    reordered = jnp.stack(
        lax.sort((inverse,) + tuple(evolved[v] for v in range(vectors)), num_keys=1)[1:], 0
    )
    leaving = (
        reordered.reshape(vectors, devices, piece_rows)
        .transpose(1, 0, 2)
        .reshape(count_first, count_second, vectors * piece_rows)
    )
    landed = lax.all_to_all(
        lax.all_to_all(leaving, "bxy", split_axis=0, concat_axis=0, tiled=True),
        "bz",
        split_axis=1,
        concat_axis=1,
        tiled=True,
    )
    work = (
        landed.reshape(count_first, count_second, vectors, piece_rows)
        .transpose(1, 2, 0, 3)
        .reshape(BLK, panel_rows)
    )
    highest = lax.Precision.HIGHEST
    proj = tree_sum(jnp.dot(basis, work.T, precision=highest), ("bz", "bxy")) / total_rows
    resid = work - jnp.dot(proj.T, basis, precision=highest)
    gram = tree_sum(jnp.dot(resid, resid.T, precision=highest), ("bz", "bxy")) / total_rows
    lower = jnp.linalg.cholesky(gram)
    ortho = lax.linalg.triangular_solve(lower, resid, left_side=True, lower=True)
    return (ortho, proj, lower.T)


def solution(mesh):
    in_specs = (
        P(None, ("bxy", "bz")),
        P(None, "bxy", None, None),
        P("bxy", None, None),
        P("bxy", None, None),
        P("bxy", None),
    )
    out_specs = (P(None, ("bxy", "bz")), P(), P())
    return jax.shard_map(body, mesh=mesh, in_specs=in_specs, out_specs=out_specs, check_vma=False)
```

```python
import jax
import jax.numpy as jnp
from jax import lax
from jax.sharding import PartitionSpec as P

BLK = 16
KB = 48
STEPS = 2


FLOW_DIRS = (
    (0, 0, 0),
    (1, 0, 0),
    (-1, 0, 0),
    (0, 1, 0),
    (0, -1, 0),
    (0, 0, 1),
    (0, 0, -1),
    (1, 1, 0),
    (-1, -1, 0),
    (1, -1, 0),
    (-1, 1, 0),
    (1, 0, 1),
    (-1, 0, -1),
    (1, 0, -1),
    (-1, 0, 1),
    (0, 1, 1),
    (0, -1, -1),
    (0, 1, -1),
    (0, -1, 1),
)
ALL_DIRS = FLOW_DIRS + FLOW_DIRS[:7]
FLOW_WEIGHTS = (1.0 / 3.0,) + (1.0 / 18.0,) * 6 + (1.0 / 36.0,) * 12
HEAT_WEIGHTS = (0.25,) + (0.125,) * 6
OPPOSITE = (0,) + tuple((number + 1 if number % 2 == 1 else number - 1 for number in range(1, 19)))
OMEGA_FLOW = 1.6
OMEGA_HEAT = 1.4
BUOYANCY = 0.2


def with_halo(block, sides, width):
    for axis, dim in sides:
        count = lax.axis_size(axis)
        forward = [(i, i + 1) for i in range(count - 1)]
        forward.append((count - 1, 0))
        backward = [(target, source) for source, target in forward]
        low = lax.ppermute(
            lax.slice_in_dim(block, block.shape[dim] - width, None, axis=dim), axis, forward
        )
        high = lax.ppermute(lax.slice_in_dim(block, 0, width, axis=dim), axis, backward)
        block = jnp.concatenate([low, block, high], axis=dim)
    return block


def tree_sum(value, axes):
    for axis in axes:
        count = lax.axis_size(axis)
        if count & (count - 1):
            value = lax.psum(value, axis)
            continue
        stride = 1
        while stride < count:
            value = value + lax.ppermute(value, axis, [(i, i ^ stride) for i in range(count)])
            stride *= 2
    return value


def along(direction, comps):
    total = 0.0
    for weight, array in zip(direction, comps):
        if weight == 1:
            total = total + array
        elif weight == -1:
            total = total - array
    return total


def moments(flow, heat):
    density = flow[0]
    for number in range(1, 19):
        density = density + flow[number]
    momentum = []
    for comp in range(3):
        momentum.append(along([FLOW_DIRS[number][comp] for number in range(19)], flow))
    warmth = heat[0]
    for number in range(1, 7):
        warmth = warmth + heat[number]
    return (density, momentum, warmth)


def equilibria(density, momentum, warmth, velocity, temper):
    carried = [momentum[comp] - velocity[comp] * density for comp in range(3)]
    speed_sq = velocity[0] * velocity[0] + velocity[1] * velocity[1] + velocity[2] * velocity[2]
    carried_u = velocity[0] * carried[0] + velocity[1] * carried[1] + velocity[2] * carried[2]
    flow_eq = []
    heat_eq = []
    for number in range(19):
        drift = along(FLOW_DIRS[number], velocity)
        push = along(FLOW_DIRS[number], carried)
        value = (
            density * (1.0 + 3.0 * drift + 4.5 * drift * drift - 1.5 * speed_sq)
            + 3.0 * push
            + 9.0 * drift * push
            - 3.0 * carried_u
        )
        flow_eq.append(FLOW_WEIGHTS[number] * value)
        if number < 7:
            heat_eq.append(
                HEAT_WEIGHTS[number] * (warmth * (1.0 + 4.0 * drift) + 4.0 * temper * push)
            )
    return (flow_eq, heat_eq)


def collide(flow, heat, velocity, temper, solid):
    density, momentum, warmth = moments(flow, heat)
    flow_eq, heat_eq = equilibria(density, momentum, warmth, velocity, temper)
    flow_new = []
    heat_new = []
    for number in range(19):
        fresh = (
            flow[number]
            - OMEGA_FLOW * (flow[number] - flow_eq[number])
            + 3.0 * FLOW_WEIGHTS[number] * FLOW_DIRS[number][1] * BUOYANCY * warmth
        )
        flow_new.append(jnp.where(solid, flow[OPPOSITE[number]], fresh))
    for number in range(7):
        fresh = heat[number] - OMEGA_HEAT * (heat[number] - heat_eq[number])
        heat_new.append(jnp.where(solid, heat[OPPOSITE[number]], fresh))
    return (flow_new, heat_new)


def stream(flow, heat):
    pops = flow + heat
    cells_first = pops[0].shape[1]
    count = lax.axis_size("bxy")
    forward = [(i, (i + 1) % count) for i in range(count)]
    backward = [((i + 1) % count, i) for i in range(count)]
    plus = [n for n in range(26) if ALL_DIRS[n][0] == 1]
    minus = [n for n in range(26) if ALL_DIRS[n][0] == -1]
    low = lax.ppermute(
        jnp.stack([pops[n][:, cells_first - 1 :] for n in plus], 1), "bxy", forward
    )
    high = lax.ppermute(jnp.stack([pops[n][:, :1] for n in minus], 1), "bxy", backward)
    moved = []
    for number in range(26):
        first, second, third = ALL_DIRS[number]
        piece = pops[number]
        if first == 1:
            piece = jnp.concatenate([low[:, plus.index(number)], piece[:, : cells_first - 1]], 1)
        elif first == -1:
            piece = jnp.concatenate([piece[:, 1:], high[:, minus.index(number)]], 1)
        moved.append(jnp.roll(piece, (second, third), axis=(2, 3)))
    return (moved[:19], moved[19:])


def body(basis, velocity, temper, flags, order):
    count_first = lax.axis_size("bxy")
    count_second = lax.axis_size("bz")
    devices = count_first * count_second
    panel_rows = basis.shape[1]
    piece_rows = panel_rows // count_first
    slab_rows = piece_rows * devices
    total_rows = panel_rows * devices
    vectors = BLK // count_second
    cells_first, cells_vertical, cells_third = temper.shape
    permute = order.reshape(slab_rows)
    block = basis[KB - BLK :]
    outgoing = (
        block.reshape(count_second, vectors, count_first, piece_rows)
        .transpose(2, 0, 1, 3)
        .reshape(count_first, count_second, vectors * piece_rows)
    )
    arrived = lax.all_to_all(
        outgoing.reshape(devices, vectors * piece_rows),
        ("bxy", "bz"),
        split_axis=0,
        concat_axis=0,
        tiled=True,
    )
    permuted = (
        arrived.reshape(devices, vectors, piece_rows).transpose(1, 0, 2).reshape(vectors, slab_rows)
    )
    ranked = lax.sort(
        (permute, lax.iota(jnp.int32, slab_rows)) + tuple(permuted[v] for v in range(vectors)),
        num_keys=1,
    )
    inverse = ranked[1]
    fields = jnp.stack(ranked[2:], 0).reshape(vectors, 5, cells_first, cells_vertical, cells_third)
    height = lax.broadcasted_iota(jnp.int32, temper.shape, 1)
    solid = (flags == 1) | (height == 0) | (height == cells_vertical - 1)
    speeds = [velocity[0], velocity[1], velocity[2]]
    flow, heat = equilibria(
        fields[:, 0], [fields[:, 1], fields[:, 2], fields[:, 3]], fields[:, 4], speeds, temper
    )
    for turn in range(STEPS):
        flow, heat = collide(flow, heat, speeds, temper, solid)
        flow, heat = stream(flow, heat)
    density, momentum, warmth = moments(flow, heat)
    evolved = jnp.stack([density] + momentum + [warmth], 1).reshape(vectors, slab_rows)
    reordered = jnp.stack(
        lax.sort((inverse,) + tuple(evolved[v] for v in range(vectors)), num_keys=1)[1:], 0
    )
    leaving = (
        reordered.reshape(vectors, devices, piece_rows)
        .transpose(1, 0, 2)
        .reshape(count_first, count_second, vectors * piece_rows)
    )
    landed = lax.all_to_all(
        leaving.reshape(devices, vectors * piece_rows),
        ("bxy", "bz"),
        split_axis=0,
        concat_axis=0,
        tiled=True,
    )
    work = (
        landed.reshape(count_first, count_second, vectors, piece_rows)
        .transpose(1, 2, 0, 3)
        .reshape(BLK, panel_rows)
    )
    highest = lax.Precision.HIGHEST
    proj = tree_sum(jnp.dot(basis, work.T, precision=highest), ("bz", "bxy")) / total_rows
    resid = work - jnp.dot(proj.T, basis, precision=highest)
    gram = tree_sum(jnp.dot(resid, resid.T, precision=highest), ("bz", "bxy")) / total_rows
    lower = jnp.linalg.cholesky(gram)
    ortho = lax.linalg.triangular_solve(lower, resid, left_side=True, lower=True)
    return (ortho, proj, lower.T)


def solution(mesh):
    in_specs = (
        P(None, ("bxy", "bz")),
        P(None, "bxy", None, None),
        P("bxy", None, None),
        P("bxy", None, None),
        P("bxy", None),
    )
    out_specs = (P(None, ("bxy", "bz")), P(), P())
    return jax.shard_map(body, mesh=mesh, in_specs=in_specs, out_specs=out_specs, check_vma=False)
```

```python
import jax
import jax.numpy as jnp
from jax import lax
from jax.sharding import PartitionSpec as P

BLK = 16
KB = 48
STEPS = 2


FLOW_DIRS = (
    (0, 0, 0),
    (1, 0, 0),
    (-1, 0, 0),
    (0, 1, 0),
    (0, -1, 0),
    (0, 0, 1),
    (0, 0, -1),
    (1, 1, 0),
    (-1, -1, 0),
    (1, -1, 0),
    (-1, 1, 0),
    (1, 0, 1),
    (-1, 0, -1),
    (1, 0, -1),
    (-1, 0, 1),
    (0, 1, 1),
    (0, -1, -1),
    (0, 1, -1),
    (0, -1, 1),
)
ALL_DIRS = FLOW_DIRS + FLOW_DIRS[:7]
FLOW_WEIGHTS = (1.0 / 3.0,) + (1.0 / 18.0,) * 6 + (1.0 / 36.0,) * 12
HEAT_WEIGHTS = (0.25,) + (0.125,) * 6
OPPOSITE = (0,) + tuple((number + 1 if number % 2 == 1 else number - 1 for number in range(1, 19)))
OMEGA_FLOW = 1.6
OMEGA_HEAT = 1.4
BUOYANCY = 0.2


def with_halo(block, sides, width):
    for axis, dim in sides:
        count = lax.axis_size(axis)
        forward = [(i, i + 1) for i in range(count - 1)]
        forward.append((count - 1, 0))
        backward = [(target, source) for source, target in forward]
        low = lax.ppermute(
            lax.slice_in_dim(block, block.shape[dim] - width, None, axis=dim), axis, forward
        )
        high = lax.ppermute(lax.slice_in_dim(block, 0, width, axis=dim), axis, backward)
        block = jnp.concatenate([low, block, high], axis=dim)
    return block


def tree_sum(value, axes):
    for axis in axes:
        count = lax.axis_size(axis)
        if count & (count - 1):
            value = lax.psum(value, axis)
            continue
        stride = 1
        while stride < count:
            value = value + lax.ppermute(value, axis, [(i, i ^ stride) for i in range(count)])
            stride *= 2
    return value


def along(direction, comps):
    total = 0.0
    for weight, array in zip(direction, comps):
        if weight == 1:
            total = total + array
        elif weight == -1:
            total = total - array
    return total


def moments(flow, heat):
    density = flow[0]
    for number in range(1, 19):
        density = density + flow[number]
    momentum = []
    for comp in range(3):
        momentum.append(along([FLOW_DIRS[number][comp] for number in range(19)], flow))
    warmth = heat[0]
    for number in range(1, 7):
        warmth = warmth + heat[number]
    return (density, momentum, warmth)


def equilibria(density, momentum, warmth, velocity, temper):
    carried = [momentum[comp] - velocity[comp] * density for comp in range(3)]
    speed_sq = velocity[0] * velocity[0] + velocity[1] * velocity[1] + velocity[2] * velocity[2]
    carried_u = velocity[0] * carried[0] + velocity[1] * carried[1] + velocity[2] * carried[2]
    flow_eq = []
    heat_eq = []
    for number in range(19):
        drift = along(FLOW_DIRS[number], velocity)
        push = along(FLOW_DIRS[number], carried)
        value = (
            density * (1.0 + 3.0 * drift + 4.5 * drift * drift - 1.5 * speed_sq)
            + 3.0 * push
            + 9.0 * drift * push
            - 3.0 * carried_u
        )
        flow_eq.append(FLOW_WEIGHTS[number] * value)
        if number < 7:
            heat_eq.append(
                HEAT_WEIGHTS[number] * (warmth * (1.0 + 4.0 * drift) + 4.0 * temper * push)
            )
    return (flow_eq, heat_eq)


def collide(flow, heat, velocity, temper, solid):
    density, momentum, warmth = moments(flow, heat)
    flow_eq, heat_eq = equilibria(density, momentum, warmth, velocity, temper)
    flow_new = []
    heat_new = []
    for number in range(19):
        fresh = (
            flow[number]
            - OMEGA_FLOW * (flow[number] - flow_eq[number])
            + 3.0 * FLOW_WEIGHTS[number] * FLOW_DIRS[number][1] * BUOYANCY * warmth
        )
        flow_new.append(jnp.where(solid, flow[OPPOSITE[number]], fresh))
    for number in range(7):
        fresh = heat[number] - OMEGA_HEAT * (heat[number] - heat_eq[number])
        heat_new.append(jnp.where(solid, heat[OPPOSITE[number]], fresh))
    return (flow_new, heat_new)


def stream(flow, heat):
    pops = flow + heat
    cells_first = pops[0].shape[1]
    count = lax.axis_size("bxy")
    forward = [(i, (i + 1) % count) for i in range(count)]
    backward = [((i + 1) % count, i) for i in range(count)]
    plus = [n for n in range(26) if ALL_DIRS[n][0] == 1]
    minus = [n for n in range(26) if ALL_DIRS[n][0] == -1]
    low = lax.ppermute(
        jnp.stack([pops[n][:, cells_first - 1 :] for n in plus], 1), "bxy", forward
    )
    high = lax.ppermute(jnp.stack([pops[n][:, :1] for n in minus], 1), "bxy", backward)
    moved = []
    for number in range(26):
        first, second, third = ALL_DIRS[number]
        piece = pops[number]
        if first == 1:
            piece = jnp.concatenate([low[:, plus.index(number)], piece[:, : cells_first - 1]], 1)
        elif first == -1:
            piece = jnp.concatenate([piece[:, 1:], high[:, minus.index(number)]], 1)
        moved.append(jnp.roll(piece, (second, third), axis=(2, 3)))
    return (moved[:19], moved[19:])


def body(basis, velocity, temper, flags, order):
    count_first = lax.axis_size("bxy")
    count_second = lax.axis_size("bz")
    devices = count_first * count_second
    panel_rows = basis.shape[1]
    piece_rows = panel_rows // count_first
    slab_rows = piece_rows * devices
    total_rows = panel_rows * devices
    vectors = BLK // count_second
    cells_first, cells_vertical, cells_third = temper.shape
    permute = order.reshape(slab_rows)
    block = basis[KB - BLK :]
    outgoing = (
        block.reshape(count_second, vectors, count_first, piece_rows)
        .transpose(2, 0, 1, 3)
        .reshape(count_first, count_second, vectors * piece_rows)
    )
    arrived = lax.all_to_all(
        outgoing.reshape(devices, vectors * piece_rows),
        ("bxy", "bz"),
        split_axis=0,
        concat_axis=0,
        tiled=True,
    )
    permuted = (
        arrived.reshape(devices, vectors, piece_rows).transpose(1, 0, 2).reshape(vectors, slab_rows)
    )
    height = lax.broadcasted_iota(jnp.int32, temper.shape, 1)
    solid = (flags == 1) | (height == 0) | (height == cells_vertical - 1)
    speeds = [velocity[0], velocity[1], velocity[2]]
    counter = lax.iota(jnp.int32, slab_rows)

    def evolve(carry):
        inverse = carry[1]
        fields = jnp.stack(carry[2:], 0).reshape(
            vectors, 5, cells_first, cells_vertical, cells_third
        )
        flow, heat = equilibria(
            fields[:, 0], [fields[:, 1], fields[:, 2], fields[:, 3]], fields[:, 4], speeds, temper
        )
        def advance(turn, populations):
            return stream(*collide(*populations, speeds, temper, solid))

        flow, heat = lax.fori_loop(0, STEPS, advance, (flow, heat))
        density, momentum, warmth = moments(flow, heat)
        evolved = jnp.stack([density] + momentum + [warmth], 1).reshape(vectors, slab_rows)
        return (inverse, counter) + tuple(evolved[v] for v in range(vectors))

    def rank(step, carry):
        ranked = tuple(lax.sort(carry, num_keys=1))
        return lax.cond(step == 0, evolve, lambda kept: kept, ranked)

    finished = lax.fori_loop(
        0, 2, rank, (permute, counter) + tuple(permuted[v] for v in range(vectors))
    )
    reordered = jnp.stack(finished[2:], 0)
    leaving = (
        reordered.reshape(vectors, devices, piece_rows)
        .transpose(1, 0, 2)
        .reshape(count_first, count_second, vectors * piece_rows)
    )
    landed = lax.all_to_all(
        leaving.reshape(devices, vectors * piece_rows),
        ("bxy", "bz"),
        split_axis=0,
        concat_axis=0,
        tiled=True,
    )
    work = (
        landed.reshape(count_first, count_second, vectors, piece_rows)
        .transpose(1, 2, 0, 3)
        .reshape(BLK, panel_rows)
    )
    highest = lax.Precision.HIGHEST
    proj = tree_sum(jnp.dot(basis, work.T, precision=highest), ("bz", "bxy")) / total_rows
    resid = work - jnp.dot(proj.T, basis, precision=highest)
    gram = tree_sum(jnp.dot(resid, resid.T, precision=highest), ("bz", "bxy")) / total_rows
    lower = jnp.linalg.cholesky(gram)
    ortho = lax.linalg.triangular_solve(lower, resid, left_side=True, lower=True)
    return (ortho, proj, lower.T)


def solution(mesh):
    in_specs = (
        P(None, ("bxy", "bz")),
        P(None, "bxy", None, None),
        P("bxy", None, None),
        P("bxy", None, None),
        P("bxy", None),
    )
    out_specs = (P(None, ("bxy", "bz")), P(), P())
    return jax.shard_map(body, mesh=mesh, in_specs=in_specs, out_specs=out_specs, check_vma=False)
```

```python
import math

import jax
import jax.numpy as jnp
from jax import lax
from jax.sharding import PartitionSpec as P

BLK = 16
KB = 48
STEPS = 2


FLOW_DIRS = (
    (0, 0, 0),
    (1, 0, 0),
    (-1, 0, 0),
    (0, 1, 0),
    (0, -1, 0),
    (0, 0, 1),
    (0, 0, -1),
    (1, 1, 0),
    (-1, -1, 0),
    (1, -1, 0),
    (-1, 1, 0),
    (1, 0, 1),
    (-1, 0, -1),
    (1, 0, -1),
    (-1, 0, 1),
    (0, 1, 1),
    (0, -1, -1),
    (0, 1, -1),
    (0, -1, 1),
)
ALL_DIRS = FLOW_DIRS + FLOW_DIRS[:7]
FLOW_WEIGHTS = (1.0 / 3.0,) + (1.0 / 18.0,) * 6 + (1.0 / 36.0,) * 12
HEAT_WEIGHTS = (0.25,) + (0.125,) * 6
OPPOSITE = (0,) + tuple((number + 1 if number % 2 == 1 else number - 1 for number in range(1, 19)))
OMEGA_FLOW = 1.6
OMEGA_HEAT = 1.4
BUOYANCY = 0.2


def with_halo(block, sides, width):
    for axis, dim in sides:
        count = lax.axis_size(axis)
        forward = [(i, i + 1) for i in range(count - 1)]
        forward.append((count - 1, 0))
        backward = [(target, source) for source, target in forward]
        low = lax.ppermute(
            lax.slice_in_dim(block, block.shape[dim] - width, None, axis=dim), axis, forward
        )
        high = lax.ppermute(lax.slice_in_dim(block, 0, width, axis=dim), axis, backward)
        block = jnp.concatenate([low, block, high], axis=dim)
    return block


AXIS_PARTS = {"bxy": ((4, 8), (8, 1)), "bz": ((4, 2), (2, 1))}
RING_OF_FOUR = (0, 1, 3, 2)


def labels(axis, count):
    parts = AXIS_PARTS.get(axis, ((count, 1),))
    if count & (count - 1) or count != math.prod(size for size, _ in parts):
        parts = ((count, 1),)
    out = []
    for index in range(count):
        label = 0
        for size, stride in parts:
            digit = (index // stride) % size
            label += (RING_OF_FOUR[digit] if size == 4 else digit) * stride
        out.append(label)
    return out


def tree_sum(value, axes):
    for axis in axes:
        count = lax.axis_size(axis)
        if count & (count - 1):
            value = lax.psum(value, axis)
            continue
        named = labels(axis, count)
        place = {label: index for index, label in enumerate(named)}
        stride = 1
        while stride < count:
            pairs = [(i, place[named[i] ^ stride]) for i in range(count)]
            value = value + lax.ppermute(value, axis, pairs)
            stride *= 2
    return value


def along(direction, comps):
    total = 0.0
    for weight, array in zip(direction, comps):
        if weight == 1:
            total = total + array
        elif weight == -1:
            total = total - array
    return total


def moments(flow, heat):
    density = flow[0]
    for number in range(1, 19):
        density = density + flow[number]
    momentum = []
    for comp in range(3):
        momentum.append(along([FLOW_DIRS[number][comp] for number in range(19)], flow))
    warmth = heat[0]
    for number in range(1, 7):
        warmth = warmth + heat[number]
    return (density, momentum, warmth)


def equilibria(density, momentum, warmth, velocity, temper):
    carried = [momentum[comp] - velocity[comp] * density for comp in range(3)]
    speed_sq = velocity[0] * velocity[0] + velocity[1] * velocity[1] + velocity[2] * velocity[2]
    carried_u = velocity[0] * carried[0] + velocity[1] * carried[1] + velocity[2] * carried[2]
    flow_eq = []
    heat_eq = []
    for number in range(19):
        drift = along(FLOW_DIRS[number], velocity)
        push = along(FLOW_DIRS[number], carried)
        value = (
            density * (1.0 + 3.0 * drift + 4.5 * drift * drift - 1.5 * speed_sq)
            + 3.0 * push
            + 9.0 * drift * push
            - 3.0 * carried_u
        )
        flow_eq.append(FLOW_WEIGHTS[number] * value)
        if number < 7:
            heat_eq.append(
                HEAT_WEIGHTS[number] * (warmth * (1.0 + 4.0 * drift) + 4.0 * temper * push)
            )
    return (flow_eq, heat_eq)


def collide(flow, heat, velocity, temper, solid):
    density, momentum, warmth = moments(flow, heat)
    flow_eq, heat_eq = equilibria(density, momentum, warmth, velocity, temper)
    flow_new = []
    heat_new = []
    for number in range(19):
        fresh = (
            flow[number]
            - OMEGA_FLOW * (flow[number] - flow_eq[number])
            + 3.0 * FLOW_WEIGHTS[number] * FLOW_DIRS[number][1] * BUOYANCY * warmth
        )
        flow_new.append(jnp.where(solid, flow[OPPOSITE[number]], fresh))
    for number in range(7):
        fresh = heat[number] - OMEGA_HEAT * (heat[number] - heat_eq[number])
        heat_new.append(jnp.where(solid, heat[OPPOSITE[number]], fresh))
    return (flow_new, heat_new)


def stream(flow, heat):
    pops = flow + heat
    cells_first = pops[0].shape[1]
    count = lax.axis_size("bxy")
    forward = [(i, (i + 1) % count) for i in range(count)]
    backward = [((i + 1) % count, i) for i in range(count)]
    plus = [n for n in range(26) if ALL_DIRS[n][0] == 1]
    minus = [n for n in range(26) if ALL_DIRS[n][0] == -1]
    low = lax.ppermute(
        jnp.stack([pops[n][:, cells_first - 1 :] for n in plus], 1), "bxy", forward
    )
    high = lax.ppermute(jnp.stack([pops[n][:, :1] for n in minus], 1), "bxy", backward)
    moved = []
    for number in range(26):
        first, second, third = ALL_DIRS[number]
        piece = pops[number]
        if first == 1:
            piece = jnp.concatenate([low[:, plus.index(number)], piece[:, : cells_first - 1]], 1)
        elif first == -1:
            piece = jnp.concatenate([piece[:, 1:], high[:, minus.index(number)]], 1)
        moved.append(jnp.roll(piece, (second, third), axis=(2, 3)))
    return (moved[:19], moved[19:])


def body(basis, velocity, temper, flags, order):
    count_first = lax.axis_size("bxy")
    count_second = lax.axis_size("bz")
    devices = count_first * count_second
    panel_rows = basis.shape[1]
    piece_rows = panel_rows // count_first
    slab_rows = piece_rows * devices
    total_rows = panel_rows * devices
    vectors = BLK // count_second
    cells_first, cells_vertical, cells_third = temper.shape
    permute = order.reshape(slab_rows)
    block = basis[KB - BLK :]
    outgoing = (
        block.reshape(count_second, vectors, count_first, piece_rows)
        .transpose(2, 0, 1, 3)
        .reshape(count_first, count_second, vectors * piece_rows)
    )
    arrived = lax.all_to_all(
        outgoing.reshape(devices, vectors * piece_rows),
        ("bxy", "bz"),
        split_axis=0,
        concat_axis=0,
        tiled=True,
    )
    permuted = (
        arrived.reshape(devices, vectors, piece_rows).transpose(1, 0, 2).reshape(vectors, slab_rows)
    )
    ranked = lax.sort(
        (permute, lax.iota(jnp.int32, slab_rows)) + tuple(permuted[v] for v in range(vectors)),
        num_keys=1,
    )
    inverse = ranked[1]
    fields = jnp.stack(ranked[2:], 0).reshape(vectors, 5, cells_first, cells_vertical, cells_third)
    height = lax.broadcasted_iota(jnp.int32, temper.shape, 1)
    solid = (flags == 1) | (height == 0) | (height == cells_vertical - 1)
    speeds = [velocity[0], velocity[1], velocity[2]]
    flow, heat = equilibria(
        fields[:, 0], [fields[:, 1], fields[:, 2], fields[:, 3]], fields[:, 4], speeds, temper
    )
    for turn in range(STEPS):
        flow, heat = collide(flow, heat, speeds, temper, solid)
        flow, heat = stream(flow, heat)
    density, momentum, warmth = moments(flow, heat)
    evolved = jnp.stack([density] + momentum + [warmth], 1).reshape(vectors, slab_rows)
    reordered = jnp.stack(
        lax.sort((inverse,) + tuple(evolved[v] for v in range(vectors)), num_keys=1)[1:], 0
    )
    leaving = (
        reordered.reshape(vectors, devices, piece_rows)
        .transpose(1, 0, 2)
        .reshape(count_first, count_second, vectors * piece_rows)
    )
    landed = lax.all_to_all(
        leaving.reshape(devices, vectors * piece_rows),
        ("bxy", "bz"),
        split_axis=0,
        concat_axis=0,
        tiled=True,
    )
    work = (
        landed.reshape(count_first, count_second, vectors, piece_rows)
        .transpose(1, 2, 0, 3)
        .reshape(BLK, panel_rows)
    )
    highest = lax.Precision.HIGHEST
    proj = tree_sum(jnp.dot(basis, work.T, precision=highest), ("bz", "bxy")) / total_rows
    resid = work - jnp.dot(proj.T, basis, precision=highest)
    gram = tree_sum(jnp.dot(resid, resid.T, precision=highest), ("bz", "bxy")) / total_rows
    lower = jnp.linalg.cholesky(gram)
    ortho = lax.linalg.triangular_solve(lower, resid, left_side=True, lower=True)
    return (ortho, proj, lower.T)


def solution(mesh):
    in_specs = (
        P(None, ("bxy", "bz")),
        P(None, "bxy", None, None),
        P("bxy", None, None),
        P("bxy", None, None),
        P("bxy", None),
    )
    out_specs = (P(None, ("bxy", "bz")), P(), P())
    return jax.shard_map(body, mesh=mesh, in_specs=in_specs, out_specs=out_specs, check_vma=False)
```

```python
import math

import jax
import jax.numpy as jnp
from jax import lax
from jax.sharding import PartitionSpec as P

BLK = 16
KB = 48
STEPS = 2


FLOW_DIRS = (
    (0, 0, 0),
    (1, 0, 0),
    (-1, 0, 0),
    (0, 1, 0),
    (0, -1, 0),
    (0, 0, 1),
    (0, 0, -1),
    (1, 1, 0),
    (-1, -1, 0),
    (1, -1, 0),
    (-1, 1, 0),
    (1, 0, 1),
    (-1, 0, -1),
    (1, 0, -1),
    (-1, 0, 1),
    (0, 1, 1),
    (0, -1, -1),
    (0, 1, -1),
    (0, -1, 1),
)
ALL_DIRS = FLOW_DIRS + FLOW_DIRS[:7]
FLOW_WEIGHTS = (1.0 / 3.0,) + (1.0 / 18.0,) * 6 + (1.0 / 36.0,) * 12
HEAT_WEIGHTS = (0.25,) + (0.125,) * 6
OPPOSITE = (0,) + tuple((number + 1 if number % 2 == 1 else number - 1 for number in range(1, 19)))
OMEGA_FLOW = 1.6
OMEGA_HEAT = 1.4
BUOYANCY = 0.2


def with_halo(block, sides, width):
    for axis, dim in sides:
        count = lax.axis_size(axis)
        forward = [(i, i + 1) for i in range(count - 1)]
        forward.append((count - 1, 0))
        backward = [(target, source) for source, target in forward]
        low = lax.ppermute(
            lax.slice_in_dim(block, block.shape[dim] - width, None, axis=dim), axis, forward
        )
        high = lax.ppermute(lax.slice_in_dim(block, 0, width, axis=dim), axis, backward)
        block = jnp.concatenate([low, block, high], axis=dim)
    return block


AXIS_PARTS = {"bxy": ((4, 8), (8, 1)), "bz": ((4, 2), (2, 1))}
RING_LABELS = {4: (0, 1, 3, 2), 8: (0, 1, 2, 3, 6, 7, 4, 5)}


def labels(axis, count):
    parts = AXIS_PARTS.get(axis, ((count, 1),))
    if count & (count - 1) or count != math.prod(size for size, _ in parts):
        parts = ((count, 1),)
    out = []
    for index in range(count):
        label = 0
        for size, stride in parts:
            digit = (index // stride) % size
            label += RING_LABELS.get(size, range(size))[digit] * stride
        out.append(label)
    return out


def tree_sum(value, axes):
    for axis in axes:
        count = lax.axis_size(axis)
        if count & (count - 1):
            value = lax.psum(value, axis)
            continue
        named = labels(axis, count)
        place = {label: index for index, label in enumerate(named)}
        stride = 1
        while stride < count:
            pairs = [(i, place[named[i] ^ stride]) for i in range(count)]
            value = value + lax.ppermute(value, axis, pairs)
            stride *= 2
    return value


def along(direction, comps):
    total = 0.0
    for weight, array in zip(direction, comps):
        if weight == 1:
            total = total + array
        elif weight == -1:
            total = total - array
    return total


def moments(flow, heat):
    density = flow[0]
    for number in range(1, 19):
        density = density + flow[number]
    momentum = []
    for comp in range(3):
        momentum.append(along([FLOW_DIRS[number][comp] for number in range(19)], flow))
    warmth = heat[0]
    for number in range(1, 7):
        warmth = warmth + heat[number]
    return (density, momentum, warmth)


def equilibria(density, momentum, warmth, velocity, temper):
    carried = [momentum[comp] - velocity[comp] * density for comp in range(3)]
    speed_sq = velocity[0] * velocity[0] + velocity[1] * velocity[1] + velocity[2] * velocity[2]
    carried_u = velocity[0] * carried[0] + velocity[1] * carried[1] + velocity[2] * carried[2]
    flow_eq = []
    heat_eq = []
    for number in range(19):
        drift = along(FLOW_DIRS[number], velocity)
        push = along(FLOW_DIRS[number], carried)
        value = (
            density * (1.0 + 3.0 * drift + 4.5 * drift * drift - 1.5 * speed_sq)
            + 3.0 * push
            + 9.0 * drift * push
            - 3.0 * carried_u
        )
        flow_eq.append(FLOW_WEIGHTS[number] * value)
        if number < 7:
            heat_eq.append(
                HEAT_WEIGHTS[number] * (warmth * (1.0 + 4.0 * drift) + 4.0 * temper * push)
            )
    return (flow_eq, heat_eq)


def collide(flow, heat, velocity, temper, solid):
    density, momentum, warmth = moments(flow, heat)
    flow_eq, heat_eq = equilibria(density, momentum, warmth, velocity, temper)
    flow_new = []
    heat_new = []
    for number in range(19):
        fresh = (
            flow[number]
            - OMEGA_FLOW * (flow[number] - flow_eq[number])
            + 3.0 * FLOW_WEIGHTS[number] * FLOW_DIRS[number][1] * BUOYANCY * warmth
        )
        flow_new.append(jnp.where(solid, flow[OPPOSITE[number]], fresh))
    for number in range(7):
        fresh = heat[number] - OMEGA_HEAT * (heat[number] - heat_eq[number])
        heat_new.append(jnp.where(solid, heat[OPPOSITE[number]], fresh))
    return (flow_new, heat_new)


def stream(flow, heat):
    pops = flow + heat
    cells_first = pops[0].shape[1]
    count = lax.axis_size("bxy")
    forward = [(i, (i + 1) % count) for i in range(count)]
    backward = [((i + 1) % count, i) for i in range(count)]
    plus = [n for n in range(26) if ALL_DIRS[n][0] == 1]
    minus = [n for n in range(26) if ALL_DIRS[n][0] == -1]
    low = lax.ppermute(
        jnp.stack([pops[n][:, cells_first - 1 :] for n in plus], 1), "bxy", forward
    )
    high = lax.ppermute(jnp.stack([pops[n][:, :1] for n in minus], 1), "bxy", backward)
    moved = []
    for number in range(26):
        first, second, third = ALL_DIRS[number]
        piece = pops[number]
        if first == 1:
            piece = jnp.concatenate([low[:, plus.index(number)], piece[:, : cells_first - 1]], 1)
        elif first == -1:
            piece = jnp.concatenate([piece[:, 1:], high[:, minus.index(number)]], 1)
        moved.append(jnp.roll(piece, (second, third), axis=(2, 3)))
    return (moved[:19], moved[19:])


def body(basis, velocity, temper, flags, order):
    count_first = lax.axis_size("bxy")
    count_second = lax.axis_size("bz")
    devices = count_first * count_second
    panel_rows = basis.shape[1]
    piece_rows = panel_rows // count_first
    slab_rows = piece_rows * devices
    total_rows = panel_rows * devices
    vectors = BLK // count_second
    cells_first, cells_vertical, cells_third = temper.shape
    permute = order.reshape(slab_rows)
    block = basis[KB - BLK :]
    outgoing = (
        block.reshape(count_second, vectors, count_first, piece_rows)
        .transpose(2, 0, 1, 3)
        .reshape(count_first, count_second, vectors * piece_rows)
    )
    arrived = lax.all_to_all(
        outgoing.reshape(devices, vectors * piece_rows),
        ("bxy", "bz"),
        split_axis=0,
        concat_axis=0,
        tiled=True,
    )
    permuted = (
        arrived.reshape(devices, vectors, piece_rows).transpose(1, 0, 2).reshape(vectors, slab_rows)
    )
    ranked = lax.sort(
        (permute, lax.iota(jnp.int32, slab_rows)) + tuple(permuted[v] for v in range(vectors)),
        num_keys=1,
    )
    inverse = ranked[1]
    fields = jnp.stack(ranked[2:], 0).reshape(vectors, 5, cells_first, cells_vertical, cells_third)
    height = lax.broadcasted_iota(jnp.int32, temper.shape, 1)
    solid = (flags == 1) | (height == 0) | (height == cells_vertical - 1)
    speeds = [velocity[0], velocity[1], velocity[2]]
    flow, heat = equilibria(
        fields[:, 0], [fields[:, 1], fields[:, 2], fields[:, 3]], fields[:, 4], speeds, temper
    )
    for turn in range(STEPS):
        flow, heat = collide(flow, heat, speeds, temper, solid)
        flow, heat = stream(flow, heat)
    density, momentum, warmth = moments(flow, heat)
    evolved = jnp.stack([density] + momentum + [warmth], 1).reshape(vectors, slab_rows)
    reordered = jnp.stack(
        lax.sort((inverse,) + tuple(evolved[v] for v in range(vectors)), num_keys=1)[1:], 0
    )
    leaving = (
        reordered.reshape(vectors, devices, piece_rows)
        .transpose(1, 0, 2)
        .reshape(count_first, count_second, vectors * piece_rows)
    )
    landed = lax.all_to_all(
        leaving.reshape(devices, vectors * piece_rows),
        ("bxy", "bz"),
        split_axis=0,
        concat_axis=0,
        tiled=True,
    )
    work = (
        landed.reshape(count_first, count_second, vectors, piece_rows)
        .transpose(1, 2, 0, 3)
        .reshape(BLK, panel_rows)
    )
    highest = lax.Precision.HIGHEST
    proj = tree_sum(jnp.dot(basis, work.T, precision=highest), ("bz", "bxy")) / total_rows
    resid = work - jnp.dot(proj.T, basis, precision=highest)
    gram = tree_sum(jnp.dot(resid, resid.T, precision=highest), ("bz", "bxy")) / total_rows
    lower = jnp.linalg.cholesky(gram)
    ortho = lax.linalg.triangular_solve(lower, resid, left_side=True, lower=True)
    return (ortho, proj, lower.T)


def solution(mesh):
    in_specs = (
        P(None, ("bxy", "bz")),
        P(None, "bxy", None, None),
        P("bxy", None, None),
        P("bxy", None, None),
        P("bxy", None),
    )
    out_specs = (P(None, ("bxy", "bz")), P(), P())
    return jax.shard_map(body, mesh=mesh, in_specs=in_specs, out_specs=out_specs, check_vma=False)
```

```python
import math

import jax
import jax.numpy as jnp
from jax import lax
from jax.sharding import PartitionSpec as P

BLK = 16
KB = 48
STEPS = 2


FLOW_DIRS = (
    (0, 0, 0),
    (1, 0, 0),
    (-1, 0, 0),
    (0, 1, 0),
    (0, -1, 0),
    (0, 0, 1),
    (0, 0, -1),
    (1, 1, 0),
    (-1, -1, 0),
    (1, -1, 0),
    (-1, 1, 0),
    (1, 0, 1),
    (-1, 0, -1),
    (1, 0, -1),
    (-1, 0, 1),
    (0, 1, 1),
    (0, -1, -1),
    (0, 1, -1),
    (0, -1, 1),
)
ALL_DIRS = FLOW_DIRS + FLOW_DIRS[:7]
FLOW_WEIGHTS = (1.0 / 3.0,) + (1.0 / 18.0,) * 6 + (1.0 / 36.0,) * 12
HEAT_WEIGHTS = (0.25,) + (0.125,) * 6
OPPOSITE = (0,) + tuple((number + 1 if number % 2 == 1 else number - 1 for number in range(1, 19)))
OMEGA_FLOW = 1.6
OMEGA_HEAT = 1.4
BUOYANCY = 0.2


def with_halo(block, sides, width):
    for axis, dim in sides:
        count = lax.axis_size(axis)
        forward = [(i, i + 1) for i in range(count - 1)]
        forward.append((count - 1, 0))
        backward = [(target, source) for source, target in forward]
        low = lax.ppermute(
            lax.slice_in_dim(block, block.shape[dim] - width, None, axis=dim), axis, forward
        )
        high = lax.ppermute(lax.slice_in_dim(block, 0, width, axis=dim), axis, backward)
        block = jnp.concatenate([low, block, high], axis=dim)
    return block


AXIS_PARTS = {"bxy": ((4, 8), (8, 1)), "bz": ((4, 2), (2, 1))}
RING_LABELS = {4: (0, 1, 3, 2), 8: (0, 1, 2, 3, 6, 7, 4, 5)}


def labels(axis, count):
    parts = AXIS_PARTS.get(axis, ((count, 1),))
    if count & (count - 1) or count != math.prod(size for size, _ in parts):
        parts = ((count, 1),)
    out = []
    for index in range(count):
        label = 0
        for size, stride in parts:
            digit = (index // stride) % size
            label += RING_LABELS.get(size, range(size))[digit] * stride
        out.append(label)
    return out


def tree_sum(value, axes):
    for axis in axes:
        count = lax.axis_size(axis)
        if count & (count - 1):
            value = lax.psum(value, axis)
            continue
        named = labels(axis, count)
        place = {label: index for index, label in enumerate(named)}
        stride = 1
        while stride < count:
            pairs = [(i, place[named[i] ^ stride]) for i in range(count)]
            value = value + lax.ppermute(value, axis, pairs)
            stride *= 2
    return value


def along(direction, comps):
    total = 0.0
    for weight, array in zip(direction, comps):
        if weight == 1:
            total = total + array
        elif weight == -1:
            total = total - array
    return total


def moments(flow, heat):
    density = flow[0]
    for number in range(1, 19):
        density = density + flow[number]
    momentum = []
    for comp in range(3):
        momentum.append(along([FLOW_DIRS[number][comp] for number in range(19)], flow))
    warmth = heat[0]
    for number in range(1, 7):
        warmth = warmth + heat[number]
    return (density, momentum, warmth)


def equilibria(density, momentum, warmth, velocity, temper):
    carried = [momentum[comp] - velocity[comp] * density for comp in range(3)]
    speed_sq = velocity[0] * velocity[0] + velocity[1] * velocity[1] + velocity[2] * velocity[2]
    carried_u = velocity[0] * carried[0] + velocity[1] * carried[1] + velocity[2] * carried[2]
    flow_eq = []
    heat_eq = []
    for number in range(19):
        drift = along(FLOW_DIRS[number], velocity)
        push = along(FLOW_DIRS[number], carried)
        value = (
            density * (1.0 + 3.0 * drift + 4.5 * drift * drift - 1.5 * speed_sq)
            + 3.0 * push
            + 9.0 * drift * push
            - 3.0 * carried_u
        )
        flow_eq.append(FLOW_WEIGHTS[number] * value)
        if number < 7:
            heat_eq.append(
                HEAT_WEIGHTS[number] * (warmth * (1.0 + 4.0 * drift) + 4.0 * temper * push)
            )
    return (flow_eq, heat_eq)


def collide(flow, heat, velocity, temper, solid):
    density, momentum, warmth = moments(flow, heat)
    flow_eq, heat_eq = equilibria(density, momentum, warmth, velocity, temper)
    flow_new = []
    heat_new = []
    for number in range(19):
        fresh = (
            flow[number]
            - OMEGA_FLOW * (flow[number] - flow_eq[number])
            + 3.0 * FLOW_WEIGHTS[number] * FLOW_DIRS[number][1] * BUOYANCY * warmth
        )
        flow_new.append(jnp.where(solid, flow[OPPOSITE[number]], fresh))
    for number in range(7):
        fresh = heat[number] - OMEGA_HEAT * (heat[number] - heat_eq[number])
        heat_new.append(jnp.where(solid, heat[OPPOSITE[number]], fresh))
    return (flow_new, heat_new)


def stream(flow, heat):
    pops = flow + heat
    cells_first = pops[0].shape[1]
    count = lax.axis_size("bxy")
    forward = [(i, (i + 1) % count) for i in range(count)]
    backward = [((i + 1) % count, i) for i in range(count)]
    plus = [n for n in range(26) if ALL_DIRS[n][0] == 1]
    minus = [n for n in range(26) if ALL_DIRS[n][0] == -1]
    low = lax.ppermute(
        jnp.stack([pops[n][:, cells_first - 1 :] for n in plus], 1), "bxy", forward
    )
    high = lax.ppermute(jnp.stack([pops[n][:, :1] for n in minus], 1), "bxy", backward)
    moved = []
    for number in range(26):
        first, second, third = ALL_DIRS[number]
        piece = pops[number]
        if first == 1:
            piece = jnp.concatenate([low[:, plus.index(number)], piece[:, : cells_first - 1]], 1)
        elif first == -1:
            piece = jnp.concatenate([piece[:, 1:], high[:, minus.index(number)]], 1)
        moved.append(jnp.roll(piece, (second, third), axis=(2, 3)))
    return (moved[:19], moved[19:])


def body(basis, velocity, temper, flags, order):
    count_first = lax.axis_size("bxy")
    count_second = lax.axis_size("bz")
    devices = count_first * count_second
    panel_rows = basis.shape[1]
    piece_rows = panel_rows // count_first
    slab_rows = piece_rows * devices
    total_rows = panel_rows * devices
    vectors = BLK // count_second
    cells_first, cells_vertical, cells_third = temper.shape
    permute = order.reshape(slab_rows)
    block = basis[KB - BLK :]
    outgoing = (
        block.reshape(count_second, vectors, count_first, piece_rows)
        .transpose(2, 0, 1, 3)
        .reshape(count_first, count_second, vectors * piece_rows)
    )
    arrived = lax.all_to_all(
        outgoing.reshape(devices, vectors, piece_rows),
        ("bxy", "bz"),
        split_axis=0,
        concat_axis=0,
        tiled=True,
    )
    permuted = (
        arrived.reshape(devices, vectors, piece_rows).transpose(1, 0, 2).reshape(vectors, slab_rows)
    )
    ranked = lax.sort(
        (permute, lax.iota(jnp.int32, slab_rows)) + tuple(permuted[v] for v in range(vectors)),
        num_keys=1,
    )
    inverse = ranked[1]
    fields = jnp.stack(ranked[2:], 0).reshape(vectors, 5, cells_first, cells_vertical, cells_third)
    height = lax.broadcasted_iota(jnp.int32, temper.shape, 1)
    solid = (flags == 1) | (height == 0) | (height == cells_vertical - 1)
    speeds = [velocity[0], velocity[1], velocity[2]]
    flow, heat = equilibria(
        fields[:, 0], [fields[:, 1], fields[:, 2], fields[:, 3]], fields[:, 4], speeds, temper
    )
    for turn in range(STEPS):
        flow, heat = collide(flow, heat, speeds, temper, solid)
        flow, heat = stream(flow, heat)
    density, momentum, warmth = moments(flow, heat)
    evolved = jnp.stack([density] + momentum + [warmth], 1).reshape(vectors, slab_rows)
    reordered = jnp.stack(
        lax.sort((inverse,) + tuple(evolved[v] for v in range(vectors)), num_keys=1)[1:], 0
    )
    leaving = (
        reordered.reshape(vectors, devices, piece_rows)
        .transpose(1, 0, 2)
        .reshape(count_first, count_second, vectors * piece_rows)
    )
    landed = lax.all_to_all(
        leaving.reshape(devices, vectors, piece_rows),
        ("bxy", "bz"),
        split_axis=0,
        concat_axis=0,
        tiled=True,
    )
    work = (
        landed.reshape(count_first, count_second, vectors, piece_rows)
        .transpose(1, 2, 0, 3)
        .reshape(BLK, panel_rows)
    )
    highest = lax.Precision.HIGHEST
    proj = tree_sum(jnp.dot(basis, work.T, precision=highest), ("bz", "bxy")) / total_rows
    resid = work - jnp.dot(proj.T, basis, precision=highest)
    gram = tree_sum(jnp.dot(resid, resid.T, precision=highest), ("bz", "bxy")) / total_rows
    lower = jnp.linalg.cholesky(gram)
    ortho = lax.linalg.triangular_solve(lower, resid, left_side=True, lower=True)
    return (ortho, proj, lower.T)


def solution(mesh):
    in_specs = (
        P(None, ("bxy", "bz")),
        P(None, "bxy", None, None),
        P("bxy", None, None),
        P("bxy", None, None),
        P("bxy", None),
    )
    out_specs = (P(None, ("bxy", "bz")), P(), P())
    return jax.shard_map(body, mesh=mesh, in_specs=in_specs, out_specs=out_specs, check_vma=False)
```

```python
import math

import jax
import jax.numpy as jnp
from jax import lax
from jax.experimental import pallas as pl
from jax.sharding import PartitionSpec as P

BLK = 16
KB = 48
STEPS = 2


FLOW_DIRS = (
    (0, 0, 0),
    (1, 0, 0),
    (-1, 0, 0),
    (0, 1, 0),
    (0, -1, 0),
    (0, 0, 1),
    (0, 0, -1),
    (1, 1, 0),
    (-1, -1, 0),
    (1, -1, 0),
    (-1, 1, 0),
    (1, 0, 1),
    (-1, 0, -1),
    (1, 0, -1),
    (-1, 0, 1),
    (0, 1, 1),
    (0, -1, -1),
    (0, 1, -1),
    (0, -1, 1),
)
ALL_DIRS = FLOW_DIRS + FLOW_DIRS[:7]
FLOW_WEIGHTS = (1.0 / 3.0,) + (1.0 / 18.0,) * 6 + (1.0 / 36.0,) * 12
HEAT_WEIGHTS = (0.25,) + (0.125,) * 6
OPPOSITE = (0,) + tuple((number + 1 if number % 2 == 1 else number - 1 for number in range(1, 19)))
OMEGA_FLOW = 1.6
OMEGA_HEAT = 1.4
BUOYANCY = 0.2


def with_halo(block, sides, width):
    for axis, dim in sides:
        count = lax.axis_size(axis)
        forward = [(i, i + 1) for i in range(count - 1)]
        forward.append((count - 1, 0))
        backward = [(target, source) for source, target in forward]
        low = lax.ppermute(
            lax.slice_in_dim(block, block.shape[dim] - width, None, axis=dim), axis, forward
        )
        high = lax.ppermute(lax.slice_in_dim(block, 0, width, axis=dim), axis, backward)
        block = jnp.concatenate([low, block, high], axis=dim)
    return block


AXIS_PARTS = {"bxy": ((4, 8), (8, 1)), "bz": ((4, 2), (2, 1))}
RING_LABELS = {4: (0, 1, 3, 2), 8: (0, 1, 2, 3, 6, 7, 4, 5)}


def labels(axis, count):
    parts = AXIS_PARTS.get(axis, ((count, 1),))
    if count & (count - 1) or count != math.prod(size for size, _ in parts):
        parts = ((count, 1),)
    out = []
    for index in range(count):
        label = 0
        for size, stride in parts:
            digit = (index // stride) % size
            label += RING_LABELS.get(size, range(size))[digit] * stride
        out.append(label)
    return out


def tree_sum(value, axes):
    for axis in axes:
        count = lax.axis_size(axis)
        if count & (count - 1):
            value = lax.psum(value, axis)
            continue
        named = labels(axis, count)
        place = {label: index for index, label in enumerate(named)}
        stride = 1
        while stride < count:
            pairs = [(i, place[named[i] ^ stride]) for i in range(count)]
            value = value + lax.ppermute(value, axis, pairs)
            stride *= 2
    return value


def along(direction, comps):
    total = 0.0
    for weight, array in zip(direction, comps):
        if weight == 1:
            total = total + array
        elif weight == -1:
            total = total - array
    return total


def moments(flow, heat):
    density = flow[0]
    for number in range(1, 19):
        density = density + flow[number]
    momentum = []
    for comp in range(3):
        momentum.append(along([FLOW_DIRS[number][comp] for number in range(19)], flow))
    warmth = heat[0]
    for number in range(1, 7):
        warmth = warmth + heat[number]
    return (density, momentum, warmth)


def equilibria(density, momentum, warmth, velocity, temper):
    carried = [momentum[comp] - velocity[comp] * density for comp in range(3)]
    speed_sq = velocity[0] * velocity[0] + velocity[1] * velocity[1] + velocity[2] * velocity[2]
    carried_u = velocity[0] * carried[0] + velocity[1] * carried[1] + velocity[2] * carried[2]
    flow_eq = []
    heat_eq = []
    for number in range(19):
        drift = along(FLOW_DIRS[number], velocity)
        push = along(FLOW_DIRS[number], carried)
        value = (
            density * (1.0 + 3.0 * drift + 4.5 * drift * drift - 1.5 * speed_sq)
            + 3.0 * push
            + 9.0 * drift * push
            - 3.0 * carried_u
        )
        flow_eq.append(FLOW_WEIGHTS[number] * value)
        if number < 7:
            heat_eq.append(
                HEAT_WEIGHTS[number] * (warmth * (1.0 + 4.0 * drift) + 4.0 * temper * push)
            )
    return (flow_eq, heat_eq)


def collide(flow, heat, velocity, temper, solid):
    density, momentum, warmth = moments(flow, heat)
    flow_eq, heat_eq = equilibria(density, momentum, warmth, velocity, temper)
    flow_new = []
    heat_new = []
    for number in range(19):
        fresh = (
            flow[number]
            - OMEGA_FLOW * (flow[number] - flow_eq[number])
            + 3.0 * FLOW_WEIGHTS[number] * FLOW_DIRS[number][1] * BUOYANCY * warmth
        )
        flow_new.append(jnp.where(solid, flow[OPPOSITE[number]], fresh))
    for number in range(7):
        fresh = heat[number] - OMEGA_HEAT * (heat[number] - heat_eq[number])
        heat_new.append(jnp.where(solid, heat[OPPOSITE[number]], fresh))
    return (flow_new, heat_new)


def stream(flow, heat):
    pops = flow + heat
    cells_first = pops[0].shape[1]
    count = lax.axis_size("bxy")
    forward = [(i, (i + 1) % count) for i in range(count)]
    backward = [((i + 1) % count, i) for i in range(count)]
    plus = [n for n in range(26) if ALL_DIRS[n][0] == 1]
    minus = [n for n in range(26) if ALL_DIRS[n][0] == -1]
    low = lax.ppermute(
        jnp.stack([pops[n][:, cells_first - 1 :] for n in plus], 1), "bxy", forward
    )
    high = lax.ppermute(jnp.stack([pops[n][:, :1] for n in minus], 1), "bxy", backward)
    moved = []
    for number in range(26):
        first, second, third = ALL_DIRS[number]
        piece = pops[number]
        if first == 1:
            piece = jnp.concatenate([low[:, plus.index(number)], piece[:, : cells_first - 1]], 1)
        elif first == -1:
            piece = jnp.concatenate([piece[:, 1:], high[:, minus.index(number)]], 1)
        moved.append(jnp.roll(piece, (second, third), axis=(2, 3)))
    return (moved[:19], moved[19:])


def factor_kernel(gram_ref, resid_ref, ortho_ref, upper_ref):
    size = gram_ref.shape[0]
    raw = gram_ref[...]
    rows = lax.broadcasted_iota(jnp.int32, (size, size), 0)
    cols = lax.broadcasted_iota(jnp.int32, (size, size), 1)
    eye = (rows == cols).astype(jnp.float32)
    exact = lax.Precision.HIGHEST
    swap = (((1,), (1,)), ((), ()))
    left = (raw + lax.dot_general(eye, raw, swap, precision=exact)) * 0.5
    lower = jnp.zeros((size, size), jnp.float32)
    for j in range(size):
        pivot = jnp.sqrt(left[j : j + 1, j : j + 1])
        column = jnp.where(rows[:, j : j + 1] >= j, left[:, j : j + 1] / pivot, 0.0)
        row = jnp.where(cols[j : j + 1, :] >= j, left[j : j + 1, :] / pivot, 0.0)
        left = left - column * row
        lower = lower + column * (cols[j : j + 1, :] == j).astype(jnp.float32)
    upper_ref[...] = lax.dot_general(eye, lower, swap, precision=exact)
    solved = resid_ref[...]
    for j in range(size):
        head = solved[j : j + 1, :] / lower[j : j + 1, j : j + 1]
        below = jnp.where(rows[:, j : j + 1] > j, lower[:, j : j + 1], 0.0)
        keep = (rows[:, j : j + 1] == j).astype(jnp.float32)
        solved = solved - below * head + keep * (head - solved[j : j + 1, :])
    ortho_ref[...] = solved


def factor(gram, resid):
    size, width = resid.shape
    return pl.pallas_call(
        factor_kernel,
        out_shape=(
            jax.ShapeDtypeStruct((size, width), jnp.float32),
            jax.ShapeDtypeStruct((size, size), jnp.float32),
        ),
    )(gram, resid)


def body(basis, velocity, temper, flags, order):
    count_first = lax.axis_size("bxy")
    count_second = lax.axis_size("bz")
    devices = count_first * count_second
    panel_rows = basis.shape[1]
    piece_rows = panel_rows // count_first
    slab_rows = piece_rows * devices
    total_rows = panel_rows * devices
    vectors = BLK // count_second
    cells_first, cells_vertical, cells_third = temper.shape
    permute = order.reshape(slab_rows)
    block = basis[KB - BLK :]
    outgoing = (
        block.reshape(count_second, vectors, count_first, piece_rows)
        .transpose(2, 0, 1, 3)
        .reshape(count_first, count_second, vectors * piece_rows)
    )
    arrived = lax.all_to_all(
        outgoing.reshape(devices, vectors, piece_rows),
        ("bxy", "bz"),
        split_axis=0,
        concat_axis=0,
        tiled=True,
    )
    permuted = (
        arrived.reshape(devices, vectors, piece_rows).transpose(1, 0, 2).reshape(vectors, slab_rows)
    )
    ranked = lax.sort(
        (permute, lax.iota(jnp.int32, slab_rows)) + tuple(permuted[v] for v in range(vectors)),
        num_keys=1,
    )
    inverse = ranked[1]
    fields = jnp.stack(ranked[2:], 0).reshape(vectors, 5, cells_first, cells_vertical, cells_third)
    height = lax.broadcasted_iota(jnp.int32, temper.shape, 1)
    solid = (flags == 1) | (height == 0) | (height == cells_vertical - 1)
    speeds = [velocity[0], velocity[1], velocity[2]]
    flow, heat = equilibria(
        fields[:, 0], [fields[:, 1], fields[:, 2], fields[:, 3]], fields[:, 4], speeds, temper
    )
    for turn in range(STEPS):
        flow, heat = collide(flow, heat, speeds, temper, solid)
        flow, heat = stream(flow, heat)
    density, momentum, warmth = moments(flow, heat)
    evolved = jnp.stack([density] + momentum + [warmth], 1).reshape(vectors, slab_rows)
    reordered = jnp.stack(
        lax.sort((inverse,) + tuple(evolved[v] for v in range(vectors)), num_keys=1)[1:], 0
    )
    leaving = (
        reordered.reshape(vectors, devices, piece_rows)
        .transpose(1, 0, 2)
        .reshape(count_first, count_second, vectors * piece_rows)
    )
    landed = lax.all_to_all(
        leaving.reshape(devices, vectors, piece_rows),
        ("bxy", "bz"),
        split_axis=0,
        concat_axis=0,
        tiled=True,
    )
    work = (
        landed.reshape(count_first, count_second, vectors, piece_rows)
        .transpose(1, 2, 0, 3)
        .reshape(BLK, panel_rows)
    )
    highest = lax.Precision.HIGHEST
    proj = tree_sum(jnp.dot(basis, work.T, precision=highest), ("bz", "bxy")) / total_rows
    resid = work - jnp.dot(proj.T, basis, precision=highest)
    gram = tree_sum(jnp.dot(resid, resid.T, precision=highest), ("bz", "bxy")) / total_rows
    ortho, upper = factor(gram, resid)
    return (ortho, proj, upper)


def solution(mesh):
    in_specs = (
        P(None, ("bxy", "bz")),
        P(None, "bxy", None, None),
        P("bxy", None, None),
        P("bxy", None, None),
        P("bxy", None),
    )
    out_specs = (P(None, ("bxy", "bz")), P(), P())
    return jax.shard_map(body, mesh=mesh, in_specs=in_specs, out_specs=out_specs, check_vma=False)
```

```python
import math

import jax
import jax.numpy as jnp
from jax import lax
from jax.experimental import pallas as pl
from jax.sharding import PartitionSpec as P

BLK = 16
KB = 48
STEPS = 2


FLOW_DIRS = (
    (0, 0, 0),
    (1, 0, 0),
    (-1, 0, 0),
    (0, 1, 0),
    (0, -1, 0),
    (0, 0, 1),
    (0, 0, -1),
    (1, 1, 0),
    (-1, -1, 0),
    (1, -1, 0),
    (-1, 1, 0),
    (1, 0, 1),
    (-1, 0, -1),
    (1, 0, -1),
    (-1, 0, 1),
    (0, 1, 1),
    (0, -1, -1),
    (0, 1, -1),
    (0, -1, 1),
)
ALL_DIRS = FLOW_DIRS + FLOW_DIRS[:7]
FLOW_WEIGHTS = (1.0 / 3.0,) + (1.0 / 18.0,) * 6 + (1.0 / 36.0,) * 12
HEAT_WEIGHTS = (0.25,) + (0.125,) * 6
OPPOSITE = (0,) + tuple((number + 1 if number % 2 == 1 else number - 1 for number in range(1, 19)))
OMEGA_FLOW = 1.6
OMEGA_HEAT = 1.4
BUOYANCY = 0.2


def with_halo(block, sides, width):
    for axis, dim in sides:
        count = lax.axis_size(axis)
        forward = [(i, i + 1) for i in range(count - 1)]
        forward.append((count - 1, 0))
        backward = [(target, source) for source, target in forward]
        low = lax.ppermute(
            lax.slice_in_dim(block, block.shape[dim] - width, None, axis=dim), axis, forward
        )
        high = lax.ppermute(lax.slice_in_dim(block, 0, width, axis=dim), axis, backward)
        block = jnp.concatenate([low, block, high], axis=dim)
    return block


AXIS_PARTS = {"bxy": ((4, 8), (8, 1)), "bz": ((4, 2), (2, 1))}
RING_LABELS = {4: (0, 1, 3, 2), 8: (0, 1, 2, 3, 6, 7, 4, 5)}


def labels(axis, count):
    parts = AXIS_PARTS.get(axis, ((count, 1),))
    if count & (count - 1) or count != math.prod(size for size, _ in parts):
        parts = ((count, 1),)
    out = []
    for index in range(count):
        label = 0
        for size, stride in parts:
            digit = (index // stride) % size
            label += RING_LABELS.get(size, range(size))[digit] * stride
        out.append(label)
    return out


def tree_sum(value, axes):
    for axis in axes:
        count = lax.axis_size(axis)
        if count & (count - 1):
            value = lax.psum(value, axis)
            continue
        named = labels(axis, count)
        place = {label: index for index, label in enumerate(named)}
        stride = 1
        while stride < count:
            pairs = [(i, place[named[i] ^ stride]) for i in range(count)]
            value = value + lax.ppermute(value, axis, pairs)
            stride *= 2
    return value


def along(direction, comps):
    total = 0.0
    for weight, array in zip(direction, comps):
        if weight == 1:
            total = total + array
        elif weight == -1:
            total = total - array
    return total


def moments(flow, heat):
    density = flow[0]
    for number in range(1, 19):
        density = density + flow[number]
    momentum = []
    for comp in range(3):
        momentum.append(along([FLOW_DIRS[number][comp] for number in range(19)], flow))
    warmth = heat[0]
    for number in range(1, 7):
        warmth = warmth + heat[number]
    return (density, momentum, warmth)


def equilibria(density, momentum, warmth, velocity, temper):
    carried = [momentum[comp] - velocity[comp] * density for comp in range(3)]
    speed_sq = velocity[0] * velocity[0] + velocity[1] * velocity[1] + velocity[2] * velocity[2]
    carried_u = velocity[0] * carried[0] + velocity[1] * carried[1] + velocity[2] * carried[2]
    flow_eq = []
    heat_eq = []
    for number in range(19):
        drift = along(FLOW_DIRS[number], velocity)
        push = along(FLOW_DIRS[number], carried)
        value = (
            density * (1.0 + 3.0 * drift + 4.5 * drift * drift - 1.5 * speed_sq)
            + 3.0 * push
            + 9.0 * drift * push
            - 3.0 * carried_u
        )
        flow_eq.append(FLOW_WEIGHTS[number] * value)
        if number < 7:
            heat_eq.append(
                HEAT_WEIGHTS[number] * (warmth * (1.0 + 4.0 * drift) + 4.0 * temper * push)
            )
    return (flow_eq, heat_eq)


def collide(flow, heat, velocity, temper, solid):
    density, momentum, warmth = moments(flow, heat)
    flow_eq, heat_eq = equilibria(density, momentum, warmth, velocity, temper)
    flow_new = []
    heat_new = []
    for number in range(19):
        fresh = (
            flow[number]
            - OMEGA_FLOW * (flow[number] - flow_eq[number])
            + 3.0 * FLOW_WEIGHTS[number] * FLOW_DIRS[number][1] * BUOYANCY * warmth
        )
        flow_new.append(jnp.where(solid, flow[OPPOSITE[number]], fresh))
    for number in range(7):
        fresh = heat[number] - OMEGA_HEAT * (heat[number] - heat_eq[number])
        heat_new.append(jnp.where(solid, heat[OPPOSITE[number]], fresh))
    return (flow_new, heat_new)


def stream(flow, heat):
    pops = flow + heat
    cells_first = pops[0].shape[1]
    count = lax.axis_size("bxy")
    forward = [(i, (i + 1) % count) for i in range(count)]
    backward = [((i + 1) % count, i) for i in range(count)]
    plus = [n for n in range(26) if ALL_DIRS[n][0] == 1]
    minus = [n for n in range(26) if ALL_DIRS[n][0] == -1]
    low = lax.ppermute(
        jnp.stack([pops[n][:, cells_first - 1 :] for n in plus], 1), "bxy", forward
    )
    high = lax.ppermute(jnp.stack([pops[n][:, :1] for n in minus], 1), "bxy", backward)
    moved = []
    for number in range(26):
        first, second, third = ALL_DIRS[number]
        piece = pops[number]
        if first == 1:
            piece = jnp.concatenate([low[:, plus.index(number)], piece[:, : cells_first - 1]], 1)
        elif first == -1:
            piece = jnp.concatenate([piece[:, 1:], high[:, minus.index(number)]], 1)
        moved.append(jnp.roll(piece, (second, third), axis=(2, 3)))
    return (moved[:19], moved[19:])


def factor_kernel(gram_ref, resid_ref, ortho_ref, upper_ref):
    size = gram_ref.shape[0]
    raw = gram_ref[...]
    rows = lax.broadcasted_iota(jnp.int32, (size, size), 0)
    cols = lax.broadcasted_iota(jnp.int32, (size, size), 1)
    eye = (rows == cols).astype(jnp.float32)
    exact = lax.Precision.HIGHEST
    swap = (((1,), (1,)), ((), ()))
    left = (raw + lax.dot_general(eye, raw, swap, precision=exact)) * 0.5
    lower = jnp.zeros((size, size), jnp.float32)
    for j in range(size):
        pivot = jnp.sqrt(left[j : j + 1, j : j + 1])
        column = jnp.where(rows[:, j : j + 1] >= j, left[:, j : j + 1] / pivot, 0.0)
        row = jnp.where(cols[j : j + 1, :] >= j, left[j : j + 1, :] / pivot, 0.0)
        left = left - column * row
        lower = lower + column * (cols[j : j + 1, :] == j).astype(jnp.float32)
    upper_ref[...] = lax.dot_general(eye, lower, swap, precision=exact)
    solved = eye
    for j in range(size):
        head = solved[j : j + 1, :] / lower[j : j + 1, j : j + 1]
        below = jnp.where(rows[:, j : j + 1] > j, lower[:, j : j + 1], 0.0)
        keep = (rows[:, j : j + 1] == j).astype(jnp.float32)
        solved = solved - below * head + keep * (head - solved[j : j + 1, :])
    ortho_ref[...] = jnp.dot(solved, resid_ref[...], precision=exact)


def factor(gram, resid):
    size, width = resid.shape
    return pl.pallas_call(
        factor_kernel,
        out_shape=(
            jax.ShapeDtypeStruct((size, width), jnp.float32),
            jax.ShapeDtypeStruct((size, size), jnp.float32),
        ),
    )(gram, resid)


def body(basis, velocity, temper, flags, order):
    count_first = lax.axis_size("bxy")
    count_second = lax.axis_size("bz")
    devices = count_first * count_second
    panel_rows = basis.shape[1]
    piece_rows = panel_rows // count_first
    slab_rows = piece_rows * devices
    total_rows = panel_rows * devices
    vectors = BLK // count_second
    cells_first, cells_vertical, cells_third = temper.shape
    permute = order.reshape(slab_rows)
    block = basis[KB - BLK :]
    outgoing = (
        block.reshape(count_second, vectors, count_first, piece_rows)
        .transpose(2, 0, 1, 3)
        .reshape(count_first, count_second, vectors * piece_rows)
    )
    arrived = lax.all_to_all(
        outgoing.reshape(devices, vectors, piece_rows),
        ("bxy", "bz"),
        split_axis=0,
        concat_axis=0,
        tiled=True,
    )
    permuted = (
        arrived.reshape(devices, vectors, piece_rows).transpose(1, 0, 2).reshape(vectors, slab_rows)
    )
    ranked = lax.sort(
        (permute, lax.iota(jnp.int32, slab_rows)) + tuple(permuted[v] for v in range(vectors)),
        num_keys=1,
    )
    inverse = ranked[1]
    fields = jnp.stack(ranked[2:], 0).reshape(vectors, 5, cells_first, cells_vertical, cells_third)
    height = lax.broadcasted_iota(jnp.int32, temper.shape, 1)
    solid = (flags == 1) | (height == 0) | (height == cells_vertical - 1)
    speeds = [velocity[0], velocity[1], velocity[2]]
    flow, heat = equilibria(
        fields[:, 0], [fields[:, 1], fields[:, 2], fields[:, 3]], fields[:, 4], speeds, temper
    )
    for turn in range(STEPS):
        flow, heat = collide(flow, heat, speeds, temper, solid)
        flow, heat = stream(flow, heat)
    density, momentum, warmth = moments(flow, heat)
    evolved = jnp.stack([density] + momentum + [warmth], 1).reshape(vectors, slab_rows)
    reordered = jnp.stack(
        lax.sort((inverse,) + tuple(evolved[v] for v in range(vectors)), num_keys=1)[1:], 0
    )
    leaving = (
        reordered.reshape(vectors, devices, piece_rows)
        .transpose(1, 0, 2)
        .reshape(count_first, count_second, vectors * piece_rows)
    )
    landed = lax.all_to_all(
        leaving.reshape(devices, vectors, piece_rows),
        ("bxy", "bz"),
        split_axis=0,
        concat_axis=0,
        tiled=True,
    )
    work = (
        landed.reshape(count_first, count_second, vectors, piece_rows)
        .transpose(1, 2, 0, 3)
        .reshape(BLK, panel_rows)
    )
    highest = lax.Precision.HIGHEST
    proj = tree_sum(jnp.dot(basis, work.T, precision=highest), ("bz", "bxy")) / total_rows
    resid = work - jnp.dot(proj.T, basis, precision=highest)
    gram = tree_sum(jnp.dot(resid, resid.T, precision=highest), ("bz", "bxy")) / total_rows
    ortho, upper = factor(gram, resid)
    return (ortho, proj, upper)


def solution(mesh):
    in_specs = (
        P(None, ("bxy", "bz")),
        P(None, "bxy", None, None),
        P("bxy", None, None),
        P("bxy", None, None),
        P("bxy", None),
    )
    out_specs = (P(None, ("bxy", "bz")), P(), P())
    return jax.shard_map(body, mesh=mesh, in_specs=in_specs, out_specs=out_specs, check_vma=False)
```

```python
import math

import jax
import jax.numpy as jnp
from jax import lax
from jax.experimental import pallas as pl
from jax.sharding import PartitionSpec as P

BLK = 16
KB = 48
STEPS = 2


FLOW_DIRS = (
    (0, 0, 0),
    (1, 0, 0),
    (-1, 0, 0),
    (0, 1, 0),
    (0, -1, 0),
    (0, 0, 1),
    (0, 0, -1),
    (1, 1, 0),
    (-1, -1, 0),
    (1, -1, 0),
    (-1, 1, 0),
    (1, 0, 1),
    (-1, 0, -1),
    (1, 0, -1),
    (-1, 0, 1),
    (0, 1, 1),
    (0, -1, -1),
    (0, 1, -1),
    (0, -1, 1),
)
ALL_DIRS = FLOW_DIRS + FLOW_DIRS[:7]
FLOW_WEIGHTS = (1.0 / 3.0,) + (1.0 / 18.0,) * 6 + (1.0 / 36.0,) * 12
HEAT_WEIGHTS = (0.25,) + (0.125,) * 6
OPPOSITE = (0,) + tuple((number + 1 if number % 2 == 1 else number - 1 for number in range(1, 19)))
OMEGA_FLOW = 1.6
OMEGA_HEAT = 1.4
BUOYANCY = 0.2


def with_halo(block, sides, width):
    for axis, dim in sides:
        count = lax.axis_size(axis)
        forward = [(i, i + 1) for i in range(count - 1)]
        forward.append((count - 1, 0))
        backward = [(target, source) for source, target in forward]
        low = lax.ppermute(
            lax.slice_in_dim(block, block.shape[dim] - width, None, axis=dim), axis, forward
        )
        high = lax.ppermute(lax.slice_in_dim(block, 0, width, axis=dim), axis, backward)
        block = jnp.concatenate([low, block, high], axis=dim)
    return block


AXIS_PARTS = {"bxy": ((4, 8), (8, 1)), "bz": ((4, 2), (2, 1))}
RING_LABELS = {4: (0, 1, 3, 2), 8: (0, 1, 2, 3, 6, 7, 4, 5)}


def labels(axis, count):
    parts = AXIS_PARTS.get(axis, ((count, 1),))
    if count & (count - 1) or count != math.prod(size for size, _ in parts):
        parts = ((count, 1),)
    out = []
    for index in range(count):
        label = 0
        for size, stride in parts:
            digit = (index // stride) % size
            label += RING_LABELS.get(size, range(size))[digit] * stride
        out.append(label)
    return out


def tree_sum(value, axes):
    for axis in axes:
        count = lax.axis_size(axis)
        if count & (count - 1):
            value = lax.psum(value, axis)
            continue
        named = labels(axis, count)
        place = {label: index for index, label in enumerate(named)}
        stride = 1
        while stride < count:
            pairs = [(i, place[named[i] ^ stride]) for i in range(count)]
            value = value + lax.ppermute(value, axis, pairs)
            stride *= 2
    return value


def along(direction, comps):
    total = 0.0
    for weight, array in zip(direction, comps):
        if weight == 1:
            total = total + array
        elif weight == -1:
            total = total - array
    return total


def moments(flow, heat):
    density = flow[0]
    for number in range(1, 19):
        density = density + flow[number]
    momentum = []
    for comp in range(3):
        momentum.append(along([FLOW_DIRS[number][comp] for number in range(19)], flow))
    warmth = heat[0]
    for number in range(1, 7):
        warmth = warmth + heat[number]
    return (density, momentum, warmth)


def equilibria(density, momentum, warmth, velocity, temper):
    carried = [momentum[comp] - velocity[comp] * density for comp in range(3)]
    speed_sq = velocity[0] * velocity[0] + velocity[1] * velocity[1] + velocity[2] * velocity[2]
    carried_u = velocity[0] * carried[0] + velocity[1] * carried[1] + velocity[2] * carried[2]
    flow_eq = []
    heat_eq = []
    for number in range(19):
        drift = along(FLOW_DIRS[number], velocity)
        push = along(FLOW_DIRS[number], carried)
        value = (
            density * (1.0 + 3.0 * drift + 4.5 * drift * drift - 1.5 * speed_sq)
            + 3.0 * push
            + 9.0 * drift * push
            - 3.0 * carried_u
        )
        flow_eq.append(FLOW_WEIGHTS[number] * value)
        if number < 7:
            heat_eq.append(
                HEAT_WEIGHTS[number] * (warmth * (1.0 + 4.0 * drift) + 4.0 * temper * push)
            )
    return (flow_eq, heat_eq)


def collide(flow, heat, velocity, temper, solid):
    density, momentum, warmth = moments(flow, heat)
    flow_eq, heat_eq = equilibria(density, momentum, warmth, velocity, temper)
    flow_new = []
    heat_new = []
    for number in range(19):
        fresh = (
            flow[number]
            - OMEGA_FLOW * (flow[number] - flow_eq[number])
            + 3.0 * FLOW_WEIGHTS[number] * FLOW_DIRS[number][1] * BUOYANCY * warmth
        )
        flow_new.append(jnp.where(solid, flow[OPPOSITE[number]], fresh))
    for number in range(7):
        fresh = heat[number] - OMEGA_HEAT * (heat[number] - heat_eq[number])
        heat_new.append(jnp.where(solid, heat[OPPOSITE[number]], fresh))
    return (flow_new, heat_new)


def stream(flow, heat):
    pops = flow + heat
    cells_first = pops[0].shape[1]
    count = lax.axis_size("bxy")
    forward = [(i, (i + 1) % count) for i in range(count)]
    backward = [((i + 1) % count, i) for i in range(count)]
    plus = [n for n in range(26) if ALL_DIRS[n][0] == 1]
    minus = [n for n in range(26) if ALL_DIRS[n][0] == -1]
    low = lax.ppermute(
        jnp.stack([pops[n][:, cells_first - 1 :] for n in plus], 1), "bxy", forward
    )
    high = lax.ppermute(jnp.stack([pops[n][:, :1] for n in minus], 1), "bxy", backward)
    moved = []
    for number in range(26):
        first, second, third = ALL_DIRS[number]
        piece = pops[number]
        if first == 1:
            piece = jnp.concatenate([low[:, plus.index(number)], piece[:, : cells_first - 1]], 1)
        elif first == -1:
            piece = jnp.concatenate([piece[:, 1:], high[:, minus.index(number)]], 1)
        moved.append(jnp.roll(piece, (second, third), axis=(2, 3)))
    return (moved[:19], moved[19:])


def final_moments(flow, heat):
    pops = flow + heat
    cells_first = pops[0].shape[1]
    count = lax.axis_size("bxy")
    forward = [(i, (i + 1) % count) for i in range(count)]
    backward = [((i + 1) % count, i) for i in range(count)]
    rolled = [jnp.roll(pops[n], ALL_DIRS[n][1:], axis=(2, 3)) for n in range(26)]

    def partial(members):
        flows = [n for n in members if n < 19]
        mass = sum(rolled[n] for n in flows)
        side = along([ALL_DIRS[n][1] for n in flows], [rolled[n] for n in flows])
        depth = along([ALL_DIRS[n][2] for n in flows], [rolled[n] for n in flows])
        warm = sum(rolled[n] for n in members if n >= 19)
        return [mass, side, depth, warm]

    still = partial([n for n in range(26) if ALL_DIRS[n][0] == 0])
    plus = jnp.stack(partial([n for n in range(26) if ALL_DIRS[n][0] == 1]), 1)
    minus = jnp.stack(partial([n for n in range(26) if ALL_DIRS[n][0] == -1]), 1)
    low = lax.ppermute(plus[:, :, cells_first - 1 :], "bxy", forward)
    high = lax.ppermute(minus[:, :, :1], "bxy", backward)
    plus = jnp.concatenate([low, plus[:, :, : cells_first - 1]], 2)
    minus = jnp.concatenate([minus[:, :, 1:], high], 2)
    density = still[0] + plus[:, 0] + minus[:, 0]
    momentum = [plus[:, 0] - minus[:, 0], still[1] + plus[:, 1] + minus[:, 1], still[2] + plus[:, 2] + minus[:, 2]]
    warmth = still[3] + plus[:, 3] + minus[:, 3]
    return (density, momentum, warmth)


def factor_kernel(gram_ref, resid_ref, ortho_ref, upper_ref):
    size = gram_ref.shape[0]
    raw = gram_ref[...]
    rows = lax.broadcasted_iota(jnp.int32, (size, size), 0)
    cols = lax.broadcasted_iota(jnp.int32, (size, size), 1)
    eye = (rows == cols).astype(jnp.float32)
    exact = lax.Precision.HIGHEST
    swap = (((1,), (1,)), ((), ()))
    left = (raw + lax.dot_general(eye, raw, swap, precision=exact)) * 0.5
    lower = jnp.zeros((size, size), jnp.float32)
    for j in range(size):
        pivot = jnp.sqrt(left[j : j + 1, j : j + 1])
        column = jnp.where(rows[:, j : j + 1] >= j, left[:, j : j + 1] / pivot, 0.0)
        row = jnp.where(cols[j : j + 1, :] >= j, left[j : j + 1, :] / pivot, 0.0)
        left = left - column * row
        lower = lower + column * (cols[j : j + 1, :] == j).astype(jnp.float32)
    upper_ref[...] = lax.dot_general(eye, lower, swap, precision=exact)
    solved = eye
    for j in range(size):
        head = solved[j : j + 1, :] / lower[j : j + 1, j : j + 1]
        below = jnp.where(rows[:, j : j + 1] > j, lower[:, j : j + 1], 0.0)
        keep = (rows[:, j : j + 1] == j).astype(jnp.float32)
        solved = solved - below * head + keep * (head - solved[j : j + 1, :])
    ortho_ref[...] = jnp.dot(solved, resid_ref[...], precision=exact)


def factor(gram, resid):
    size, width = resid.shape
    return pl.pallas_call(
        factor_kernel,
        out_shape=(
            jax.ShapeDtypeStruct((size, width), jnp.float32),
            jax.ShapeDtypeStruct((size, size), jnp.float32),
        ),
    )(gram, resid)


def body(basis, velocity, temper, flags, order):
    count_first = lax.axis_size("bxy")
    count_second = lax.axis_size("bz")
    devices = count_first * count_second
    panel_rows = basis.shape[1]
    piece_rows = panel_rows // count_first
    slab_rows = piece_rows * devices
    total_rows = panel_rows * devices
    vectors = BLK // count_second
    cells_first, cells_vertical, cells_third = temper.shape
    permute = order.reshape(slab_rows)
    block = basis[KB - BLK :]
    outgoing = (
        block.reshape(count_second, vectors, count_first, piece_rows)
        .transpose(2, 0, 1, 3)
        .reshape(count_first, count_second, vectors * piece_rows)
    )
    arrived = lax.all_to_all(
        outgoing.reshape(devices, vectors, piece_rows),
        ("bxy", "bz"),
        split_axis=0,
        concat_axis=0,
        tiled=True,
    )
    permuted = (
        arrived.reshape(devices, vectors, piece_rows).transpose(1, 0, 2).reshape(vectors, slab_rows)
    )
    ranked = lax.sort(
        (permute, lax.iota(jnp.int32, slab_rows)) + tuple(permuted[v] for v in range(vectors)),
        num_keys=1,
    )
    inverse = ranked[1]
    fields = jnp.stack(ranked[2:], 0).reshape(vectors, 5, cells_first, cells_vertical, cells_third)
    height = lax.broadcasted_iota(jnp.int32, temper.shape, 1)
    solid = (flags == 1) | (height == 0) | (height == cells_vertical - 1)
    speeds = [velocity[0], velocity[1], velocity[2]]
    flow, heat = equilibria(
        fields[:, 0], [fields[:, 1], fields[:, 2], fields[:, 3]], fields[:, 4], speeds, temper
    )
    for turn in range(STEPS - 1):
        flow, heat = collide(flow, heat, speeds, temper, solid)
        flow, heat = stream(flow, heat)
    flow, heat = collide(flow, heat, speeds, temper, solid)
    density, momentum, warmth = final_moments(flow, heat)
    evolved = jnp.stack([density] + momentum + [warmth], 1).reshape(vectors, slab_rows)
    reordered = jnp.stack(
        lax.sort((inverse,) + tuple(evolved[v] for v in range(vectors)), num_keys=1)[1:], 0
    )
    leaving = (
        reordered.reshape(vectors, devices, piece_rows)
        .transpose(1, 0, 2)
        .reshape(count_first, count_second, vectors * piece_rows)
    )
    landed = lax.all_to_all(
        leaving.reshape(devices, vectors, piece_rows),
        ("bxy", "bz"),
        split_axis=0,
        concat_axis=0,
        tiled=True,
    )
    work = (
        landed.reshape(count_first, count_second, vectors, piece_rows)
        .transpose(1, 2, 0, 3)
        .reshape(BLK, panel_rows)
    )
    highest = lax.Precision.HIGHEST
    proj = tree_sum(jnp.dot(basis, work.T, precision=highest), ("bz", "bxy")) / total_rows
    resid = work - jnp.dot(proj.T, basis, precision=highest)
    gram = tree_sum(jnp.dot(resid, resid.T, precision=highest), ("bz", "bxy")) / total_rows
    ortho, upper = factor(gram, resid)
    return (ortho, proj, upper)


def solution(mesh):
    in_specs = (
        P(None, ("bxy", "bz")),
        P(None, "bxy", None, None),
        P("bxy", None, None),
        P("bxy", None, None),
        P("bxy", None),
    )
    out_specs = (P(None, ("bxy", "bz")), P(), P())
    return jax.shard_map(body, mesh=mesh, in_specs=in_specs, out_specs=out_specs, check_vma=False)
```

```python
import math

import jax
import jax.numpy as jnp
from jax import lax
from jax.experimental import pallas as pl
from jax.sharding import PartitionSpec as P

BLK = 16
KB = 48
STEPS = 2


FLOW_DIRS = (
    (0, 0, 0),
    (1, 0, 0),
    (-1, 0, 0),
    (0, 1, 0),
    (0, -1, 0),
    (0, 0, 1),
    (0, 0, -1),
    (1, 1, 0),
    (-1, -1, 0),
    (1, -1, 0),
    (-1, 1, 0),
    (1, 0, 1),
    (-1, 0, -1),
    (1, 0, -1),
    (-1, 0, 1),
    (0, 1, 1),
    (0, -1, -1),
    (0, 1, -1),
    (0, -1, 1),
)
ALL_DIRS = FLOW_DIRS + FLOW_DIRS[:7]
FLOW_WEIGHTS = (1.0 / 3.0,) + (1.0 / 18.0,) * 6 + (1.0 / 36.0,) * 12
HEAT_WEIGHTS = (0.25,) + (0.125,) * 6
OPPOSITE = (0,) + tuple((number + 1 if number % 2 == 1 else number - 1 for number in range(1, 19)))
OMEGA_FLOW = 1.6
OMEGA_HEAT = 1.4
BUOYANCY = 0.2


def with_halo(block, sides, width):
    for axis, dim in sides:
        count = lax.axis_size(axis)
        forward = [(i, i + 1) for i in range(count - 1)]
        forward.append((count - 1, 0))
        backward = [(target, source) for source, target in forward]
        low = lax.ppermute(
            lax.slice_in_dim(block, block.shape[dim] - width, None, axis=dim), axis, forward
        )
        high = lax.ppermute(lax.slice_in_dim(block, 0, width, axis=dim), axis, backward)
        block = jnp.concatenate([low, block, high], axis=dim)
    return block


AXIS_PARTS = {"bxy": ((4, 8), (8, 1)), "bz": ((4, 2), (2, 1))}
RING_LABELS = {4: (0, 1, 3, 2), 8: (0, 1, 2, 3, 6, 7, 4, 5)}


def labels(axis, count):
    parts = AXIS_PARTS.get(axis, ((count, 1),))
    if count & (count - 1) or count != math.prod(size for size, _ in parts):
        parts = ((count, 1),)
    out = []
    for index in range(count):
        label = 0
        for size, stride in parts:
            digit = (index // stride) % size
            label += RING_LABELS.get(size, range(size))[digit] * stride
        out.append(label)
    return out


def tree_sum(value, axes):
    for axis in axes:
        count = lax.axis_size(axis)
        if count & (count - 1):
            value = lax.psum(value, axis)
            continue
        named = labels(axis, count)
        place = {label: index for index, label in enumerate(named)}
        stride = 1
        while stride < count:
            pairs = [(i, place[named[i] ^ stride]) for i in range(count)]
            value = value + lax.ppermute(value, axis, pairs)
            stride *= 2
    return value


def along(direction, comps):
    total = 0.0
    for weight, array in zip(direction, comps):
        if weight == 1:
            total = total + array
        elif weight == -1:
            total = total - array
    return total


def moments(flow, heat):
    density = flow[0]
    for number in range(1, 19):
        density = density + flow[number]
    momentum = []
    for comp in range(3):
        momentum.append(along([FLOW_DIRS[number][comp] for number in range(19)], flow))
    warmth = heat[0]
    for number in range(1, 7):
        warmth = warmth + heat[number]
    return (density, momentum, warmth)


def equilibria(density, momentum, warmth, velocity, temper):
    carried = [momentum[comp] - velocity[comp] * density for comp in range(3)]
    speed_sq = velocity[0] * velocity[0] + velocity[1] * velocity[1] + velocity[2] * velocity[2]
    carried_u = velocity[0] * carried[0] + velocity[1] * carried[1] + velocity[2] * carried[2]
    flow_eq = []
    heat_eq = []
    for number in range(19):
        drift = along(FLOW_DIRS[number], velocity)
        push = along(FLOW_DIRS[number], carried)
        value = (
            density * (1.0 + 3.0 * drift + 4.5 * drift * drift - 1.5 * speed_sq)
            + 3.0 * push
            + 9.0 * drift * push
            - 3.0 * carried_u
        )
        flow_eq.append(FLOW_WEIGHTS[number] * value)
        if number < 7:
            heat_eq.append(
                HEAT_WEIGHTS[number] * (warmth * (1.0 + 4.0 * drift) + 4.0 * temper * push)
            )
    return (flow_eq, heat_eq)


def collide(flow, heat, velocity, temper, solid):
    density, momentum, warmth = moments(flow, heat)
    flow_eq, heat_eq = equilibria(density, momentum, warmth, velocity, temper)
    flow_new = []
    heat_new = []
    for number in range(19):
        fresh = (
            flow[number]
            - OMEGA_FLOW * (flow[number] - flow_eq[number])
            + 3.0 * FLOW_WEIGHTS[number] * FLOW_DIRS[number][1] * BUOYANCY * warmth
        )
        flow_new.append(jnp.where(solid, flow[OPPOSITE[number]], fresh))
    for number in range(7):
        fresh = heat[number] - OMEGA_HEAT * (heat[number] - heat_eq[number])
        heat_new.append(jnp.where(solid, heat[OPPOSITE[number]], fresh))
    return (flow_new, heat_new)


def stream(flow, heat):
    pops = flow + heat
    cells_first = pops[0].shape[1]
    count = lax.axis_size("bxy")
    forward = [(i, (i + 1) % count) for i in range(count)]
    backward = [((i + 1) % count, i) for i in range(count)]
    plus = [n for n in range(26) if ALL_DIRS[n][0] == 1]
    minus = [n for n in range(26) if ALL_DIRS[n][0] == -1]
    low = lax.ppermute(
        jnp.stack([pops[n][:, cells_first - 1 :] for n in plus], 1), "bxy", forward
    )
    high = lax.ppermute(jnp.stack([pops[n][:, :1] for n in minus], 1), "bxy", backward)
    moved = []
    for number in range(26):
        first, second, third = ALL_DIRS[number]
        piece = pops[number]
        if first == 1:
            piece = jnp.concatenate([low[:, plus.index(number)], piece[:, : cells_first - 1]], 1)
        elif first == -1:
            piece = jnp.concatenate([piece[:, 1:], high[:, minus.index(number)]], 1)
        moved.append(jnp.roll(piece, (second, third), axis=(2, 3)))
    return (moved[:19], moved[19:])


def factor_kernel(gram_ref, resid_ref, ortho_ref, upper_ref):
    size = gram_ref.shape[0]
    raw = gram_ref[...]
    rows = lax.broadcasted_iota(jnp.int32, (size, size), 0)
    cols = lax.broadcasted_iota(jnp.int32, (size, size), 1)
    eye = (rows == cols).astype(jnp.float32)
    exact = lax.Precision.HIGHEST
    swap = (((1,), (1,)), ((), ()))
    left = (raw + lax.dot_general(eye, raw, swap, precision=exact)) * 0.5
    lower = jnp.zeros((size, size), jnp.float32)
    for j in range(size):
        scale = 1.0 / jnp.sqrt(left[j : j + 1, j : j + 1])
        column = jnp.where(rows[:, j : j + 1] >= j, left[:, j : j + 1] * scale, 0.0)
        row = jnp.where(cols[j : j + 1, :] >= j, left[j : j + 1, :] * scale, 0.0)
        left = left - column * row
        lower = lower + column * (cols[j : j + 1, :] == j).astype(jnp.float32)
    upper_ref[...] = lax.dot_general(eye, lower, swap, precision=exact)
    solved = eye
    for j in range(size):
        head = solved[j : j + 1, :] / lower[j : j + 1, j : j + 1]
        below = jnp.where(rows[:, j : j + 1] > j, lower[:, j : j + 1], 0.0)
        keep = (rows[:, j : j + 1] == j).astype(jnp.float32)
        solved = solved - below * head + keep * (head - solved[j : j + 1, :])
    ortho_ref[...] = jnp.dot(solved, resid_ref[...], precision=exact)


def factor(gram, resid):
    size, width = resid.shape
    return pl.pallas_call(
        factor_kernel,
        out_shape=(
            jax.ShapeDtypeStruct((size, width), jnp.float32),
            jax.ShapeDtypeStruct((size, size), jnp.float32),
        ),
    )(gram, resid)


def body(basis, velocity, temper, flags, order):
    count_first = lax.axis_size("bxy")
    count_second = lax.axis_size("bz")
    devices = count_first * count_second
    panel_rows = basis.shape[1]
    piece_rows = panel_rows // count_first
    slab_rows = piece_rows * devices
    total_rows = panel_rows * devices
    vectors = BLK // count_second
    cells_first, cells_vertical, cells_third = temper.shape
    permute = order.reshape(slab_rows)
    outgoing = (
        basis.reshape(KB // BLK, count_second, vectors, count_first, piece_rows)[-1]
        .transpose(2, 0, 1, 3)
        .reshape(count_first, count_second, vectors * piece_rows)
    )
    arrived = lax.all_to_all(
        outgoing.reshape(devices, vectors, piece_rows),
        ("bxy", "bz"),
        split_axis=0,
        concat_axis=0,
        tiled=True,
    )
    permuted = (
        arrived.reshape(devices, vectors, piece_rows).transpose(1, 0, 2).reshape(vectors, slab_rows)
    )
    ranked = lax.sort(
        (permute, lax.iota(jnp.int32, slab_rows)) + tuple(permuted[v] for v in range(vectors)),
        num_keys=1,
    )
    inverse = ranked[1]
    fields = jnp.stack(ranked[2:], 0).reshape(vectors, 5, cells_first, cells_vertical, cells_third)
    height = lax.broadcasted_iota(jnp.int32, temper.shape, 1)
    solid = (flags == 1) | (height == 0) | (height == cells_vertical - 1)
    speeds = [velocity[0], velocity[1], velocity[2]]
    flow, heat = equilibria(
        fields[:, 0], [fields[:, 1], fields[:, 2], fields[:, 3]], fields[:, 4], speeds, temper
    )
    for turn in range(STEPS):
        flow, heat = collide(flow, heat, speeds, temper, solid)
        flow, heat = stream(flow, heat)
    density, momentum, warmth = moments(flow, heat)
    evolved = jnp.stack([density] + momentum + [warmth], 1).reshape(vectors, slab_rows)
    reordered = jnp.stack(
        lax.sort((inverse,) + tuple(evolved[v] for v in range(vectors)), num_keys=1)[1:], 0
    )
    leaving = (
        reordered.reshape(vectors, devices, piece_rows)
        .transpose(1, 0, 2)
        .reshape(count_first, count_second, vectors * piece_rows)
    )
    landed = lax.all_to_all(
        leaving.reshape(devices, vectors, piece_rows),
        ("bxy", "bz"),
        split_axis=0,
        concat_axis=0,
        tiled=True,
    )
    work = (
        landed.reshape(count_first, count_second, vectors, piece_rows)
        .transpose(1, 2, 0, 3)
        .reshape(BLK, panel_rows)
    )
    highest = lax.Precision.HIGHEST
    proj = tree_sum(jnp.dot(basis, work.T, precision=highest), ("bz", "bxy")) / total_rows
    resid = work - jnp.dot(proj.T, basis, precision=highest)
    gram = tree_sum(jnp.dot(resid, resid.T, precision=highest), ("bz", "bxy")) / total_rows
    ortho, upper = factor(gram, resid)
    return (ortho, proj, upper)


def solution(mesh):
    in_specs = (
        P(None, ("bxy", "bz")),
        P(None, "bxy", None, None),
        P("bxy", None, None),
        P("bxy", None, None),
        P("bxy", None),
    )
    out_specs = (P(None, ("bxy", "bz")), P(), P())
    return jax.shard_map(body, mesh=mesh, in_specs=in_specs, out_specs=out_specs, check_vma=False)
```

```python
import math

import jax
import jax.numpy as jnp
from jax import lax
from jax.experimental import pallas as pl
from jax.sharding import PartitionSpec as P

BLK = 16
KB = 48
STEPS = 2


FLOW_DIRS = (
    (0, 0, 0),
    (1, 0, 0),
    (-1, 0, 0),
    (0, 1, 0),
    (0, -1, 0),
    (0, 0, 1),
    (0, 0, -1),
    (1, 1, 0),
    (-1, -1, 0),
    (1, -1, 0),
    (-1, 1, 0),
    (1, 0, 1),
    (-1, 0, -1),
    (1, 0, -1),
    (-1, 0, 1),
    (0, 1, 1),
    (0, -1, -1),
    (0, 1, -1),
    (0, -1, 1),
)
ALL_DIRS = FLOW_DIRS + FLOW_DIRS[:7]
FLOW_WEIGHTS = (1.0 / 3.0,) + (1.0 / 18.0,) * 6 + (1.0 / 36.0,) * 12
HEAT_WEIGHTS = (0.25,) + (0.125,) * 6
OPPOSITE = (0,) + tuple((number + 1 if number % 2 == 1 else number - 1 for number in range(1, 19)))
OMEGA_FLOW = 1.6
OMEGA_HEAT = 1.4
BUOYANCY = 0.2


def with_halo(block, sides, width):
    for axis, dim in sides:
        count = lax.axis_size(axis)
        forward = [(i, i + 1) for i in range(count - 1)]
        forward.append((count - 1, 0))
        backward = [(target, source) for source, target in forward]
        low = lax.ppermute(
            lax.slice_in_dim(block, block.shape[dim] - width, None, axis=dim), axis, forward
        )
        high = lax.ppermute(lax.slice_in_dim(block, 0, width, axis=dim), axis, backward)
        block = jnp.concatenate([low, block, high], axis=dim)
    return block


AXIS_PARTS = {"bxy": ((4, 8), (8, 1)), "bz": ((4, 2), (2, 1))}
RING_LABELS = {4: (0, 1, 3, 2), 8: (0, 1, 2, 3, 6, 7, 4, 5)}


def labels(axis, count):
    parts = AXIS_PARTS.get(axis, ((count, 1),))
    if count & (count - 1) or count != math.prod(size for size, _ in parts):
        parts = ((count, 1),)
    out = []
    for index in range(count):
        label = 0
        for size, stride in parts:
            digit = (index // stride) % size
            label += RING_LABELS.get(size, range(size))[digit] * stride
        out.append(label)
    return out


def tree_sum(value, axes):
    for axis in axes:
        count = lax.axis_size(axis)
        if count & (count - 1):
            value = lax.psum(value, axis)
            continue
        named = labels(axis, count)
        place = {label: index for index, label in enumerate(named)}
        stride = 1
        while stride < count:
            pairs = [(i, place[named[i] ^ stride]) for i in range(count)]
            value = value + lax.ppermute(value, axis, pairs)
            stride *= 2
    return value


def along(direction, comps):
    total = 0.0
    for weight, array in zip(direction, comps):
        if weight == 1:
            total = total + array
        elif weight == -1:
            total = total - array
    return total


def moments(flow, heat):
    density = flow[0]
    for number in range(1, 19):
        density = density + flow[number]
    momentum = []
    for comp in range(3):
        momentum.append(along([FLOW_DIRS[number][comp] for number in range(19)], flow))
    warmth = heat[0]
    for number in range(1, 7):
        warmth = warmth + heat[number]
    return (density, momentum, warmth)


def equilibria(density, momentum, warmth, velocity, temper):
    carried = [momentum[comp] - velocity[comp] * density for comp in range(3)]
    speed_sq = velocity[0] * velocity[0] + velocity[1] * velocity[1] + velocity[2] * velocity[2]
    carried_u = velocity[0] * carried[0] + velocity[1] * carried[1] + velocity[2] * carried[2]
    flow_eq = []
    heat_eq = []
    for number in range(19):
        drift = along(FLOW_DIRS[number], velocity)
        push = along(FLOW_DIRS[number], carried)
        value = (
            density * (1.0 + 3.0 * drift + 4.5 * drift * drift - 1.5 * speed_sq)
            + 3.0 * push
            + 9.0 * drift * push
            - 3.0 * carried_u
        )
        flow_eq.append(FLOW_WEIGHTS[number] * value)
        if number < 7:
            heat_eq.append(
                HEAT_WEIGHTS[number] * (warmth * (1.0 + 4.0 * drift) + 4.0 * temper * push)
            )
    return (flow_eq, heat_eq)


def collide(flow, heat, velocity, temper, solid):
    density, momentum, warmth = moments(flow, heat)
    flow_eq, heat_eq = equilibria(density, momentum, warmth, velocity, temper)
    flow_new = []
    heat_new = []
    for number in range(19):
        fresh = (
            flow[number]
            - OMEGA_FLOW * (flow[number] - flow_eq[number])
            + 3.0 * FLOW_WEIGHTS[number] * FLOW_DIRS[number][1] * BUOYANCY * warmth
        )
        flow_new.append(jnp.where(solid, flow[OPPOSITE[number]], fresh))
    for number in range(7):
        fresh = heat[number] - OMEGA_HEAT * (heat[number] - heat_eq[number])
        heat_new.append(jnp.where(solid, heat[OPPOSITE[number]], fresh))
    return (flow_new, heat_new)


def stream(flow, heat):
    pops = flow + heat
    cells_first = pops[0].shape[1]
    count = lax.axis_size("bxy")
    forward = [(i, (i + 1) % count) for i in range(count)]
    backward = [((i + 1) % count, i) for i in range(count)]
    plus = [n for n in range(26) if ALL_DIRS[n][0] == 1]
    minus = [n for n in range(26) if ALL_DIRS[n][0] == -1]
    low = lax.ppermute(
        jnp.stack([pops[n][:, cells_first - 1 :] for n in plus], 1), "bxy", forward
    )
    high = lax.ppermute(jnp.stack([pops[n][:, :1] for n in minus], 1), "bxy", backward)
    moved = []
    for number in range(26):
        first, second, third = ALL_DIRS[number]
        piece = pops[number]
        if first == 1:
            piece = jnp.concatenate([low[:, plus.index(number)], piece[:, : cells_first - 1]], 1)
        elif first == -1:
            piece = jnp.concatenate([piece[:, 1:], high[:, minus.index(number)]], 1)
        moved.append(jnp.roll(piece, (second, third), axis=(2, 3)))
    return (moved[:19], moved[19:])


def factor_kernel(gram_ref, resid_ref, ortho_ref, upper_ref):
    size = gram_ref.shape[0]
    raw = gram_ref[...]
    rows = lax.broadcasted_iota(jnp.int32, (size, size), 0)
    cols = lax.broadcasted_iota(jnp.int32, (size, size), 1)
    eye = (rows == cols).astype(jnp.float32)
    exact = lax.Precision.HIGHEST
    swap = (((1,), (1,)), ((), ()))
    left = (raw + lax.dot_general(eye, raw, swap, precision=exact)) * 0.5
    lower = jnp.zeros((size, size), jnp.float32)
    upper = jnp.zeros((size, size), jnp.float32)
    for j in range(size):
        scale = 1.0 / jnp.sqrt(left[j : j + 1, j : j + 1])
        column = jnp.where(rows[:, j : j + 1] >= j, left[:, j : j + 1] * scale, 0.0)
        row = jnp.where(cols[j : j + 1, :] >= j, left[j : j + 1, :] * scale, 0.0)
        left = left - column * row
        lower = lower + column * (cols[j : j + 1, :] == j).astype(jnp.float32)
        upper = upper + (rows[:, j : j + 1] == j).astype(jnp.float32) * row
    upper_ref[...] = upper
    solved = eye
    for j in range(size):
        head = solved[j : j + 1, :] / lower[j : j + 1, j : j + 1]
        below = jnp.where(rows[:, j : j + 1] > j, lower[:, j : j + 1], 0.0)
        keep = (rows[:, j : j + 1] == j).astype(jnp.float32)
        solved = solved - below * head + keep * (head - solved[j : j + 1, :])
    ortho_ref[...] = jnp.dot(solved, resid_ref[...], precision=exact)


def factor(gram, resid):
    size, width = resid.shape
    return pl.pallas_call(
        factor_kernel,
        out_shape=(
            jax.ShapeDtypeStruct((size, width), jnp.float32),
            jax.ShapeDtypeStruct((size, size), jnp.float32),
        ),
    )(gram, resid)


def body(basis, velocity, temper, flags, order):
    count_first = lax.axis_size("bxy")
    count_second = lax.axis_size("bz")
    devices = count_first * count_second
    panel_rows = basis.shape[1]
    piece_rows = panel_rows // count_first
    slab_rows = piece_rows * devices
    total_rows = panel_rows * devices
    vectors = BLK // count_second
    cells_first, cells_vertical, cells_third = temper.shape
    permute = order.reshape(slab_rows)
    outgoing = (
        basis.reshape(KB // BLK, count_second, vectors, count_first, piece_rows)[-1]
        .transpose(2, 0, 1, 3)
        .reshape(count_first, count_second, vectors * piece_rows)
    )
    arrived = lax.all_to_all(
        outgoing.reshape(devices, vectors, piece_rows),
        ("bxy", "bz"),
        split_axis=0,
        concat_axis=0,
        tiled=True,
    )
    permuted = (
        arrived.reshape(devices, vectors, piece_rows).transpose(1, 0, 2).reshape(vectors, slab_rows)
    )
    ranked = lax.sort(
        (permute, lax.iota(jnp.int32, slab_rows)) + tuple(permuted[v] for v in range(vectors)),
        num_keys=1,
    )
    inverse = ranked[1]
    fields = jnp.stack(ranked[2:], 0).reshape(vectors, 5, cells_first, cells_vertical, cells_third)
    height = lax.broadcasted_iota(jnp.int32, temper.shape, 1)
    solid = (flags == 1) | (height == 0) | (height == cells_vertical - 1)
    speeds = [velocity[0], velocity[1], velocity[2]]
    flow, heat = equilibria(
        fields[:, 0], [fields[:, 1], fields[:, 2], fields[:, 3]], fields[:, 4], speeds, temper
    )
    for turn in range(STEPS):
        flow, heat = collide(flow, heat, speeds, temper, solid)
        flow, heat = stream(flow, heat)
    density, momentum, warmth = moments(flow, heat)
    evolved = jnp.stack([density] + momentum + [warmth], 1).reshape(vectors, slab_rows)
    reordered = jnp.stack(
        lax.sort((inverse,) + tuple(evolved[v] for v in range(vectors)), num_keys=1)[1:], 0
    )
    leaving = (
        reordered.reshape(vectors, devices, piece_rows)
        .transpose(1, 0, 2)
        .reshape(count_first, count_second, vectors * piece_rows)
    )
    landed = lax.all_to_all(
        leaving.reshape(devices, vectors, piece_rows),
        ("bxy", "bz"),
        split_axis=0,
        concat_axis=0,
        tiled=True,
    )
    work = (
        landed.reshape(count_first, count_second, vectors, piece_rows)
        .transpose(1, 2, 0, 3)
        .reshape(BLK, panel_rows)
    )
    highest = lax.Precision.HIGHEST
    proj = tree_sum(jnp.dot(basis, work.T, precision=highest), ("bz", "bxy")) / total_rows
    resid = work - jnp.dot(proj.T, basis, precision=highest)
    gram = tree_sum(jnp.dot(resid, resid.T, precision=highest), ("bz", "bxy")) / total_rows
    ortho, upper = factor(gram, resid)
    return (ortho, proj, upper)


def solution(mesh):
    in_specs = (
        P(None, ("bxy", "bz")),
        P(None, "bxy", None, None),
        P("bxy", None, None),
        P("bxy", None, None),
        P("bxy", None),
    )
    out_specs = (P(None, ("bxy", "bz")), P(), P())
    return jax.shard_map(body, mesh=mesh, in_specs=in_specs, out_specs=out_specs, check_vma=False)
```

```python
import math

import jax
import jax.numpy as jnp
from jax import lax
from jax.experimental import pallas as pl
from jax.sharding import PartitionSpec as P

BLK = 16
KB = 48
STEPS = 2


FLOW_DIRS = (
    (0, 0, 0),
    (1, 0, 0),
    (-1, 0, 0),
    (0, 1, 0),
    (0, -1, 0),
    (0, 0, 1),
    (0, 0, -1),
    (1, 1, 0),
    (-1, -1, 0),
    (1, -1, 0),
    (-1, 1, 0),
    (1, 0, 1),
    (-1, 0, -1),
    (1, 0, -1),
    (-1, 0, 1),
    (0, 1, 1),
    (0, -1, -1),
    (0, 1, -1),
    (0, -1, 1),
)
ALL_DIRS = FLOW_DIRS + FLOW_DIRS[:7]
FLOW_WEIGHTS = (1.0 / 3.0,) + (1.0 / 18.0,) * 6 + (1.0 / 36.0,) * 12
HEAT_WEIGHTS = (0.25,) + (0.125,) * 6
OPPOSITE = (0,) + tuple((number + 1 if number % 2 == 1 else number - 1 for number in range(1, 19)))
OMEGA_FLOW = 1.6
OMEGA_HEAT = 1.4
BUOYANCY = 0.2


def with_halo(block, sides, width):
    for axis, dim in sides:
        count = lax.axis_size(axis)
        forward = [(i, i + 1) for i in range(count - 1)]
        forward.append((count - 1, 0))
        backward = [(target, source) for source, target in forward]
        low = lax.ppermute(
            lax.slice_in_dim(block, block.shape[dim] - width, None, axis=dim), axis, forward
        )
        high = lax.ppermute(lax.slice_in_dim(block, 0, width, axis=dim), axis, backward)
        block = jnp.concatenate([low, block, high], axis=dim)
    return block


AXIS_PARTS = {"bxy": ((4, 8), (8, 1)), "bz": ((4, 2), (2, 1))}
RING_LABELS = {4: (0, 1, 3, 2), 8: (0, 1, 2, 3, 6, 7, 4, 5)}


def labels(axis, count):
    parts = AXIS_PARTS.get(axis, ((count, 1),))
    if count & (count - 1) or count != math.prod(size for size, _ in parts):
        parts = ((count, 1),)
    out = []
    for index in range(count):
        label = 0
        for size, stride in parts:
            digit = (index // stride) % size
            label += RING_LABELS.get(size, range(size))[digit] * stride
        out.append(label)
    return out


def tree_sum(value, axes):
    for axis in axes:
        count = lax.axis_size(axis)
        if count & (count - 1):
            value = lax.psum(value, axis)
            continue
        named = labels(axis, count)
        place = {label: index for index, label in enumerate(named)}
        stride = 1
        while stride < count:
            pairs = [(i, place[named[i] ^ stride]) for i in range(count)]
            value = value + lax.ppermute(value, axis, pairs)
            stride *= 2
    return value


def along(direction, comps):
    total = 0.0
    for weight, array in zip(direction, comps):
        if weight == 1:
            total = total + array
        elif weight == -1:
            total = total - array
    return total


def moments(flow, heat):
    density = flow[0]
    for number in range(1, 19):
        density = density + flow[number]
    momentum = []
    for comp in range(3):
        momentum.append(along([FLOW_DIRS[number][comp] for number in range(19)], flow))
    warmth = heat[0]
    for number in range(1, 7):
        warmth = warmth + heat[number]
    return (density, momentum, warmth)


def equilibria(density, momentum, warmth, velocity, temper):
    carried = [momentum[comp] - velocity[comp] * density for comp in range(3)]
    speed_sq = velocity[0] * velocity[0] + velocity[1] * velocity[1] + velocity[2] * velocity[2]
    carried_u = velocity[0] * carried[0] + velocity[1] * carried[1] + velocity[2] * carried[2]
    flow_eq = []
    heat_eq = []
    for number in range(19):
        drift = along(FLOW_DIRS[number], velocity)
        push = along(FLOW_DIRS[number], carried)
        value = (
            density * (1.0 + 3.0 * drift + 4.5 * drift * drift - 1.5 * speed_sq)
            + 3.0 * push
            + 9.0 * drift * push
            - 3.0 * carried_u
        )
        flow_eq.append(FLOW_WEIGHTS[number] * value)
        if number < 7:
            heat_eq.append(
                HEAT_WEIGHTS[number] * (warmth * (1.0 + 4.0 * drift) + 4.0 * temper * push)
            )
    return (flow_eq, heat_eq)


def collide(flow, heat, velocity, temper, solid):
    density, momentum, warmth = moments(flow, heat)
    flow_eq, heat_eq = equilibria(density, momentum, warmth, velocity, temper)
    flow_new = []
    heat_new = []
    for number in range(19):
        fresh = (
            flow[number]
            - OMEGA_FLOW * (flow[number] - flow_eq[number])
            + 3.0 * FLOW_WEIGHTS[number] * FLOW_DIRS[number][1] * BUOYANCY * warmth
        )
        flow_new.append(jnp.where(solid, flow[OPPOSITE[number]], fresh))
    for number in range(7):
        fresh = heat[number] - OMEGA_HEAT * (heat[number] - heat_eq[number])
        heat_new.append(jnp.where(solid, heat[OPPOSITE[number]], fresh))
    return (flow_new, heat_new)


def stream(flow, heat):
    pops = flow + heat
    cells_first = pops[0].shape[1]
    count = lax.axis_size("bxy")
    forward = [(i, (i + 1) % count) for i in range(count)]
    backward = [((i + 1) % count, i) for i in range(count)]
    plus = [n for n in range(26) if ALL_DIRS[n][0] == 1]
    minus = [n for n in range(26) if ALL_DIRS[n][0] == -1]
    low = lax.ppermute(
        jnp.stack([pops[n][:, cells_first - 1 :] for n in plus], 1), "bxy", forward
    )
    high = lax.ppermute(jnp.stack([pops[n][:, :1] for n in minus], 1), "bxy", backward)
    moved = []
    for number in range(26):
        first, second, third = ALL_DIRS[number]
        piece = pops[number]
        if first == 1:
            piece = jnp.concatenate([low[:, plus.index(number)], piece[:, : cells_first - 1]], 1)
        elif first == -1:
            piece = jnp.concatenate([piece[:, 1:], high[:, minus.index(number)]], 1)
        moved.append(jnp.roll(piece, (second, third), axis=(2, 3)))
    return (moved[:19], moved[19:])


def factor_kernel(gram_ref, resid_ref, ortho_ref, upper_ref):
    size = gram_ref.shape[0]
    raw = gram_ref[...]
    rows = lax.broadcasted_iota(jnp.int32, (size, size), 0)
    cols = lax.broadcasted_iota(jnp.int32, (size, size), 1)
    eye = (rows == cols).astype(jnp.float32)
    exact = lax.Precision.HIGHEST
    left = raw
    lower = jnp.zeros((size, size), jnp.float32)
    upper = jnp.zeros((size, size), jnp.float32)
    for j in range(size):
        scale = 1.0 / jnp.sqrt(left[j : j + 1, j : j + 1])
        column = jnp.where(rows[:, j : j + 1] >= j, left[:, j : j + 1] * scale, 0.0)
        row = jnp.where(cols[j : j + 1, :] >= j, left[j : j + 1, :] * scale, 0.0)
        left = left - column * row
        lower = lower + column * (cols[j : j + 1, :] == j).astype(jnp.float32)
        upper = upper + (rows[:, j : j + 1] == j).astype(jnp.float32) * row
    upper_ref[...] = upper
    solved = eye
    for j in range(size):
        head = solved[j : j + 1, :] / lower[j : j + 1, j : j + 1]
        below = jnp.where(rows[:, j : j + 1] > j, lower[:, j : j + 1], 0.0)
        keep = (rows[:, j : j + 1] == j).astype(jnp.float32)
        solved = solved - below * head + keep * (head - solved[j : j + 1, :])
    ortho_ref[...] = jnp.dot(solved, resid_ref[...], precision=exact)


def factor(gram, resid):
    size, width = resid.shape
    return pl.pallas_call(
        factor_kernel,
        out_shape=(
            jax.ShapeDtypeStruct((size, width), jnp.float32),
            jax.ShapeDtypeStruct((size, size), jnp.float32),
        ),
    )(gram, resid)


def body(basis, velocity, temper, flags, order):
    count_first = lax.axis_size("bxy")
    count_second = lax.axis_size("bz")
    devices = count_first * count_second
    panel_rows = basis.shape[1]
    piece_rows = panel_rows // count_first
    slab_rows = piece_rows * devices
    total_rows = panel_rows * devices
    vectors = BLK // count_second
    cells_first, cells_vertical, cells_third = temper.shape
    permute = order.reshape(slab_rows)
    outgoing = (
        basis.reshape(KB // BLK, count_second, vectors, count_first, piece_rows)[-1]
        .transpose(2, 0, 1, 3)
        .reshape(count_first, count_second, vectors * piece_rows)
    )
    arrived = lax.all_to_all(
        outgoing.reshape(devices, vectors, piece_rows),
        ("bxy", "bz"),
        split_axis=0,
        concat_axis=0,
        tiled=True,
    )
    permuted = (
        arrived.reshape(devices, vectors, piece_rows).transpose(1, 0, 2).reshape(vectors, slab_rows)
    )
    ranked = lax.sort(
        (permute, lax.iota(jnp.int32, slab_rows)) + tuple(permuted[v] for v in range(vectors)),
        num_keys=1,
    )
    inverse = ranked[1]
    fields = jnp.stack(ranked[2:], 0).reshape(vectors, 5, cells_first, cells_vertical, cells_third)
    height = lax.broadcasted_iota(jnp.int32, temper.shape, 1)
    solid = (flags == 1) | (height == 0) | (height == cells_vertical - 1)
    speeds = [velocity[0], velocity[1], velocity[2]]
    flow, heat = equilibria(
        fields[:, 0], [fields[:, 1], fields[:, 2], fields[:, 3]], fields[:, 4], speeds, temper
    )
    for turn in range(STEPS):
        flow, heat = collide(flow, heat, speeds, temper, solid)
        flow, heat = stream(flow, heat)
    density, momentum, warmth = moments(flow, heat)
    evolved = jnp.stack([density] + momentum + [warmth], 1).reshape(vectors, slab_rows)
    reordered = jnp.stack(
        lax.sort((inverse,) + tuple(evolved[v] for v in range(vectors)), num_keys=1)[1:], 0
    )
    leaving = (
        reordered.reshape(vectors, devices, piece_rows)
        .transpose(1, 0, 2)
        .reshape(count_first, count_second, vectors * piece_rows)
    )
    landed = lax.all_to_all(
        leaving.reshape(devices, vectors, piece_rows),
        ("bxy", "bz"),
        split_axis=0,
        concat_axis=0,
        tiled=True,
    )
    work = (
        landed.reshape(count_first, count_second, vectors, piece_rows)
        .transpose(1, 2, 0, 3)
        .reshape(BLK, panel_rows)
    )
    highest = lax.Precision.HIGHEST
    proj = tree_sum(jnp.dot(basis, work.T, precision=highest), ("bz", "bxy")) / total_rows
    resid = work - jnp.dot(proj.T, basis, precision=highest)
    gram = tree_sum(jnp.dot(resid, resid.T, precision=highest), ("bz", "bxy")) / total_rows
    ortho, upper = factor((gram + gram.T) * 0.5, resid)
    return (ortho, proj, upper)


def solution(mesh):
    in_specs = (
        P(None, ("bxy", "bz")),
        P(None, "bxy", None, None),
        P("bxy", None, None),
        P("bxy", None, None),
        P("bxy", None),
    )
    out_specs = (P(None, ("bxy", "bz")), P(), P())
    return jax.shard_map(body, mesh=mesh, in_specs=in_specs, out_specs=out_specs, check_vma=False)
```

```python
import math

import jax
import jax.numpy as jnp
from jax import lax
from jax.experimental import pallas as pl
from jax.sharding import PartitionSpec as P

BLK = 16
KB = 48
STEPS = 2


FLOW_DIRS = (
    (0, 0, 0),
    (1, 0, 0),
    (-1, 0, 0),
    (0, 1, 0),
    (0, -1, 0),
    (0, 0, 1),
    (0, 0, -1),
    (1, 1, 0),
    (-1, -1, 0),
    (1, -1, 0),
    (-1, 1, 0),
    (1, 0, 1),
    (-1, 0, -1),
    (1, 0, -1),
    (-1, 0, 1),
    (0, 1, 1),
    (0, -1, -1),
    (0, 1, -1),
    (0, -1, 1),
)
ALL_DIRS = FLOW_DIRS + FLOW_DIRS[:7]
FLOW_WEIGHTS = (1.0 / 3.0,) + (1.0 / 18.0,) * 6 + (1.0 / 36.0,) * 12
HEAT_WEIGHTS = (0.25,) + (0.125,) * 6
OPPOSITE = (0,) + tuple((number + 1 if number % 2 == 1 else number - 1 for number in range(1, 19)))
OMEGA_FLOW = 1.6
OMEGA_HEAT = 1.4
BUOYANCY = 0.2


def with_halo(block, sides, width):
    for axis, dim in sides:
        count = lax.axis_size(axis)
        forward = [(i, i + 1) for i in range(count - 1)]
        forward.append((count - 1, 0))
        backward = [(target, source) for source, target in forward]
        low = lax.ppermute(
            lax.slice_in_dim(block, block.shape[dim] - width, None, axis=dim), axis, forward
        )
        high = lax.ppermute(lax.slice_in_dim(block, 0, width, axis=dim), axis, backward)
        block = jnp.concatenate([low, block, high], axis=dim)
    return block


AXIS_PARTS = {"bxy": ((4, 8), (8, 1)), "bz": ((4, 2), (2, 1))}
RING_LABELS = {4: (0, 1, 3, 2), 8: (0, 1, 2, 3, 6, 7, 4, 5)}


def labels(axis, count):
    parts = AXIS_PARTS.get(axis, ((count, 1),))
    if count & (count - 1) or count != math.prod(size for size, _ in parts):
        parts = ((count, 1),)
    out = []
    for index in range(count):
        label = 0
        for size, stride in parts:
            digit = (index // stride) % size
            label += RING_LABELS.get(size, range(size))[digit] * stride
        out.append(label)
    return out


def tree_sum(value, axes):
    for axis in axes:
        count = lax.axis_size(axis)
        if count & (count - 1):
            value = lax.psum(value, axis)
            continue
        named = labels(axis, count)
        place = {label: index for index, label in enumerate(named)}
        stride = 1
        while stride < count:
            pairs = [(i, place[named[i] ^ stride]) for i in range(count)]
            value = value + lax.ppermute(value, axis, pairs)
            stride *= 2
    return value


def along(direction, comps):
    total = 0.0
    for weight, array in zip(direction, comps):
        if weight == 1:
            total = total + array
        elif weight == -1:
            total = total - array
    return total


def moments(flow, heat):
    density = flow[0]
    for number in range(1, 19):
        density = density + flow[number]
    momentum = []
    for comp in range(3):
        momentum.append(along([FLOW_DIRS[number][comp] for number in range(19)], flow))
    warmth = heat[0]
    for number in range(1, 7):
        warmth = warmth + heat[number]
    return (density, momentum, warmth)


def equilibria(density, momentum, warmth, velocity, temper):
    carried = [momentum[comp] - velocity[comp] * density for comp in range(3)]
    speed_sq = velocity[0] * velocity[0] + velocity[1] * velocity[1] + velocity[2] * velocity[2]
    carried_u = velocity[0] * carried[0] + velocity[1] * carried[1] + velocity[2] * carried[2]
    flow_eq = []
    heat_eq = []
    for number in range(19):
        drift = along(FLOW_DIRS[number], velocity)
        push = along(FLOW_DIRS[number], carried)
        value = (
            density * (1.0 + 3.0 * drift + 4.5 * drift * drift - 1.5 * speed_sq)
            + 3.0 * push
            + 9.0 * drift * push
            - 3.0 * carried_u
        )
        flow_eq.append(FLOW_WEIGHTS[number] * value)
        if number < 7:
            heat_eq.append(
                HEAT_WEIGHTS[number] * (warmth * (1.0 + 4.0 * drift) + 4.0 * temper * push)
            )
    return (flow_eq, heat_eq)


def collide(flow, heat, velocity, temper, solid):
    density, momentum, warmth = moments(flow, heat)
    flow_eq, heat_eq = equilibria(density, momentum, warmth, velocity, temper)
    flow_new = []
    heat_new = []
    for number in range(19):
        fresh = (
            flow[number]
            - OMEGA_FLOW * (flow[number] - flow_eq[number])
            + 3.0 * FLOW_WEIGHTS[number] * FLOW_DIRS[number][1] * BUOYANCY * warmth
        )
        flow_new.append(jnp.where(solid, flow[OPPOSITE[number]], fresh))
    for number in range(7):
        fresh = heat[number] - OMEGA_HEAT * (heat[number] - heat_eq[number])
        heat_new.append(jnp.where(solid, heat[OPPOSITE[number]], fresh))
    return (flow_new, heat_new)


def stream(flow, heat):
    pops = flow + heat
    cells_first = pops[0].shape[1]
    count = lax.axis_size("bxy")
    forward = [(i, (i + 1) % count) for i in range(count)]
    backward = [((i + 1) % count, i) for i in range(count)]
    plus = [n for n in range(26) if ALL_DIRS[n][0] == 1]
    minus = [n for n in range(26) if ALL_DIRS[n][0] == -1]
    low = lax.ppermute(
        jnp.stack([pops[n][:, cells_first - 1 :] for n in plus], 1), "bxy", forward
    )
    high = lax.ppermute(jnp.stack([pops[n][:, :1] for n in minus], 1), "bxy", backward)
    moved = []
    for number in range(26):
        first, second, third = ALL_DIRS[number]
        piece = pops[number]
        if first == 1:
            piece = jnp.concatenate([low[:, plus.index(number)], piece[:, : cells_first - 1]], 1)
        elif first == -1:
            piece = jnp.concatenate([piece[:, 1:], high[:, minus.index(number)]], 1)
        moved.append(jnp.roll(piece, (second, third), axis=(2, 3)))
    return (moved[:19], moved[19:])


def factor_kernel(gram_ref, resid_ref, ortho_ref, upper_ref):
    size = gram_ref.shape[0]
    raw = gram_ref[...]
    rows = lax.broadcasted_iota(jnp.int32, (size, size), 0)
    cols = lax.broadcasted_iota(jnp.int32, (size, size), 1)
    eye = (rows == cols).astype(jnp.float32)
    exact = lax.Precision.HIGHEST
    swap = (((1,), (1,)), ((), ()))
    left = (raw + lax.dot_general(eye, raw, swap, precision=exact)) * 0.5
    lower = jnp.zeros((size, size), jnp.float32)
    upper = jnp.zeros((size, size), jnp.float32)
    scales = []
    for j in range(size):
        scale = 1.0 / jnp.sqrt(left[j : j + 1, j : j + 1])
        scales.append(scale)
        column = jnp.where(rows[:, j : j + 1] >= j, left[:, j : j + 1] * scale, 0.0)
        row = jnp.where(cols[j : j + 1, :] >= j, left[j : j + 1, :] * scale, 0.0)
        left = left - column * row
        lower = lower + column * (cols[j : j + 1, :] == j).astype(jnp.float32)
        upper = upper + (rows[:, j : j + 1] == j).astype(jnp.float32) * row
    upper_ref[...] = upper
    solved = eye
    for j in range(size):
        head = solved[j : j + 1, :] * scales[j]
        below = jnp.where(rows[:, j : j + 1] > j, lower[:, j : j + 1], 0.0)
        keep = (rows[:, j : j + 1] == j).astype(jnp.float32)
        solved = solved - below * head + keep * (head - solved[j : j + 1, :])
    ortho_ref[...] = jnp.dot(solved, resid_ref[...], precision=exact)


def factor(gram, resid):
    size, width = resid.shape
    return pl.pallas_call(
        factor_kernel,
        out_shape=(
            jax.ShapeDtypeStruct((size, width), jnp.float32),
            jax.ShapeDtypeStruct((size, size), jnp.float32),
        ),
    )(gram, resid)


def body(basis, velocity, temper, flags, order):
    count_first = lax.axis_size("bxy")
    count_second = lax.axis_size("bz")
    devices = count_first * count_second
    panel_rows = basis.shape[1]
    piece_rows = panel_rows // count_first
    slab_rows = piece_rows * devices
    total_rows = panel_rows * devices
    vectors = BLK // count_second
    cells_first, cells_vertical, cells_third = temper.shape
    permute = order.reshape(slab_rows)
    outgoing = (
        basis.reshape(KB // BLK, count_second, vectors, count_first, piece_rows)[-1]
        .transpose(2, 0, 1, 3)
        .reshape(count_first, count_second, vectors * piece_rows)
    )
    arrived = lax.all_to_all(
        outgoing.reshape(devices, vectors, piece_rows),
        ("bxy", "bz"),
        split_axis=0,
        concat_axis=0,
        tiled=True,
    )
    permuted = (
        arrived.reshape(devices, vectors, piece_rows).transpose(1, 0, 2).reshape(vectors, slab_rows)
    )
    ranked = lax.sort(
        (permute, lax.iota(jnp.int32, slab_rows)) + tuple(permuted[v] for v in range(vectors)),
        num_keys=1,
    )
    inverse = ranked[1]
    fields = jnp.stack(ranked[2:], 0).reshape(vectors, 5, cells_first, cells_vertical, cells_third)
    height = lax.broadcasted_iota(jnp.int32, temper.shape, 1)
    solid = (flags == 1) | (height == 0) | (height == cells_vertical - 1)
    speeds = [velocity[0], velocity[1], velocity[2]]
    flow, heat = equilibria(
        fields[:, 0], [fields[:, 1], fields[:, 2], fields[:, 3]], fields[:, 4], speeds, temper
    )
    for turn in range(STEPS):
        flow, heat = collide(flow, heat, speeds, temper, solid)
        flow, heat = stream(flow, heat)
    density, momentum, warmth = moments(flow, heat)
    evolved = jnp.stack([density] + momentum + [warmth], 1).reshape(vectors, slab_rows)
    reordered = jnp.stack(
        lax.sort((inverse,) + tuple(evolved[v] for v in range(vectors)), num_keys=1)[1:], 0
    )
    leaving = (
        reordered.reshape(vectors, devices, piece_rows)
        .transpose(1, 0, 2)
        .reshape(count_first, count_second, vectors * piece_rows)
    )
    landed = lax.all_to_all(
        leaving.reshape(devices, vectors, piece_rows),
        ("bxy", "bz"),
        split_axis=0,
        concat_axis=0,
        tiled=True,
    )
    work = (
        landed.reshape(count_first, count_second, vectors, piece_rows)
        .transpose(1, 2, 0, 3)
        .reshape(BLK, panel_rows)
    )
    highest = lax.Precision.HIGHEST
    proj = tree_sum(jnp.dot(basis, work.T, precision=highest), ("bz", "bxy")) / total_rows
    resid = work - jnp.dot(proj.T, basis, precision=highest)
    gram = tree_sum(jnp.dot(resid, resid.T, precision=highest), ("bz", "bxy")) / total_rows
    ortho, upper = factor(gram, resid)
    return (ortho, proj, upper)


def solution(mesh):
    in_specs = (
        P(None, ("bxy", "bz")),
        P(None, "bxy", None, None),
        P("bxy", None, None),
        P("bxy", None, None),
        P("bxy", None),
    )
    out_specs = (P(None, ("bxy", "bz")), P(), P())
    return jax.shard_map(body, mesh=mesh, in_specs=in_specs, out_specs=out_specs, check_vma=False)
```
